128 devices in a mesh: seq: 16 (over x, z_lo, core), chan: 8 (over y, z_hi).
Axes of the slice: x: 4, y: 4, z: 4 (z_hi: 2, z_lo: 2; z = z_hi * 2 + z_lo), core: 2. Of those that a mesh axis runs over, the one named last changes fastest.
Arguments:
- gate_in: bfloat16 [8192, 2048], P('seq', 'chan'), may hold values from -6 to 6
- out_gate: bfloat16 [8192, 2048], P('seq', 'chan'), may hold values from -6 to 6
- value_in: bfloat16 [8192, 2048], P('seq', 'chan'), may hold values from -6 to 6
- out_grad: bfloat16 [8192, 2048], P('seq', 'chan'), may hold values from -6 to 6
- skip_gain: float32 [2048], P('chan'), may hold values from -1 to 1
- filter_taps: float32 [8192, 256], P('seq'), may hold values from -0.0625 to 0.0625
Outputs:
- grad_gate: bfloat16 [8192, 2048], P('seq', 'chan')
- grad_out_gate: bfloat16 [8192, 2048], P('seq', 'chan')
- grad_value: bfloat16 [8192, 2048], P('seq', 'chan')
- skip_grad: float32 [2048], P('chan')
- taps_grad: float32 [8192, 256], P('seq')
The draws below stay inside these ranges and needn't reach their ends.
All inputs are finite; a program needn't handle non-finite values.
Results may differ from the reference program's by a relative error of at most 0.0052.
Values sent between devices are 32-bit elements; how exact they have to be, the bound alone decides.
No kernel may reach another device: no remote copies, remote signals or barrier semaphores. Data moves between devices by JAX's collectives and lax.ppermute only.
A program may use at most 128 MiB of HBM per device.

```python
import jax
import jax.numpy as jnp
from jax import lax

SEQ = 8192
CHANNELS = 2048
FILTERS = 256


def shard_levels(stream_key, extent, shards, smallest, top_value):
    level, own = 1.0, jax.random.fold_in(stream_key, 6)
    for axis_at, parts in shards:
        steps = jnp.exp(jax.random.uniform(jax.random.fold_in(own, axis_at), (parts,), jnp.float32, smallest / len(shards), top_value / len(shards)))
        level = level * jnp.repeat(steps, extent[axis_at] // parts).reshape([-1 if axis == axis_at else 1 for axis in range(len(extent))])
    return level


def centred(rng, extent, scale, limit, split=(), kind=jnp.bfloat16):
    array = scale * jax.random.normal(rng, extent, jnp.float32)
    if split:
        array = array * shard_levels(rng, extent, split, -0.22, 0.18)
    return jnp.clip(array, -limit, limit).astype(kind)


def setup_inputs(seed: int = 0) -> dict:
    streams_of = jax.random.split(jax.random.key(seed), 7)
    gate_in = centred(streams_of[0], (SEQ, CHANNELS), 1.0, 6.0, ((0, 16), (1, 8)))
    out_gate = centred(streams_of[1], (SEQ, CHANNELS), 1.0, 6.0, ((0, 16), (1, 8)))
    value_in = centred(streams_of[2], (SEQ, CHANNELS), 1.0, 6.0, ((0, 16), (1, 8)))
    out_grad = centred(streams_of[3], (SEQ, CHANNELS), 1.0, 6.0, ((0, 16), (1, 8)))
    skip_gain = jnp.clip(jax.random.uniform(streams_of[4], (CHANNELS,), jnp.float32, -1.0, 1.0) * shard_levels(streams_of[4], (CHANNELS,), ((0, 8),), -0.4, 0.0), -1.0, 1.0)
    filter_taps = centred(streams_of[5], (SEQ, FILTERS), SEQ ** -0.5, 0.0625, ((0, 16),), jnp.float32)
    return dict(gate_in=gate_in, out_gate=out_gate, value_in=value_in, out_grad=out_grad, skip_gain=skip_gain, filter_taps=filter_taps)


def reference(gate_in, out_gate, value_in, out_grad, skip_gain, filter_taps):
    copies = CHANNELS // FILTERS
    filt_all = jnp.tile(filter_taps, (1, copies))
    mixed_bf = lax.optimization_barrier((gate_in.astype(jnp.float32) * value_in.astype(jnp.float32)).astype(jnp.bfloat16))
    mixed_in = mixed_bf.astype(jnp.float32)
    gated_bf = lax.optimization_barrier((out_grad.astype(jnp.float32) * out_gate.astype(jnp.float32)).astype(jnp.bfloat16))
    gated_grad = gated_bf.astype(jnp.float32)
    padding = ((0, SEQ), (0, 0))
    spec_mixed = jnp.fft.fft(jnp.pad(mixed_in, padding), axis=0)
    spec_gated = jnp.fft.fft(jnp.pad(gated_grad, padding), axis=0)
    spec_filt = jnp.fft.fft(jnp.pad(filt_all, padding), axis=0)
    conv = jnp.real(jnp.fft.ifft(spec_filt * spec_mixed, axis=0)[:SEQ])
    corr = jnp.real(jnp.fft.ifft(spec_gated * jnp.conj(spec_filt), axis=0)[:SEQ])
    filt_grad = jnp.real(jnp.fft.ifft(spec_gated * jnp.conj(spec_mixed), axis=0)[:SEQ])
    out32 = out_grad.astype(jnp.float32)
    grad_out_gate = (out32 * (conv + skip_gain[None] * mixed_in)).astype(jnp.bfloat16)
    mix_grad = corr + skip_gain[None] * gated_grad
    grad_gate = (mix_grad * value_in.astype(jnp.float32)).astype(jnp.bfloat16)
    grad_value = (mix_grad * gate_in.astype(jnp.float32)).astype(jnp.bfloat16)
    skip_grad = jnp.sum(gated_grad * mixed_in, axis=0)
    taps_grad = jnp.sum(filt_grad.reshape(SEQ, copies, FILTERS), axis=1)
    return grad_gate, grad_out_gate, grad_value, skip_grad, taps_grad
```

```python
import math

import jax
import jax.numpy as jnp
from jax import lax
from jax.sharding import PartitionSpec as P

HIGHEST = lax.Precision.HIGHEST
F32 = jnp.float32


def trig(a_count, b_count, period, scale=1.0):
    a_ids = lax.iota(jnp.int32, a_count)[:, None]
    b_ids = lax.iota(jnp.int32, b_count)[None, :]
    turns = (a_ids * b_ids) % period
    angle = turns.astype(F32) * (2.0 * math.pi / period)
    return jnp.cos(angle) * scale, jnp.sin(angle) * scale


def mm(a, b):
    return jnp.dot(a, b, precision=HIGHEST, preferred_element_type=F32)


def forward_spectrum(x, blocks, rows, w1, tw_c, tw_s, w2):
    ch = x.shape[1]
    k1 = blocks + 1
    a = mm(w1, x.reshape(blocks, ch * rows)).reshape(2, k1, ch, rows)
    are, aim = a[0], a[1]
    tre = are * tw_c + aim * tw_s
    tim = aim * tw_c - are * tw_s
    b = mm(jnp.stack([tre, tim]).reshape(2 * k1 * ch, rows), w2).reshape(2, k1, ch, 2, rows)
    xre = b[0, :, :, 0] + b[1, :, :, 1]
    xim = b[1, :, :, 0] - b[0, :, :, 1]
    return xre, xim


def inverse_real(yre, yim, blocks, rows, w2, tw_c, tw_s, wi):
    k1, ch = yre.shape[0], yre.shape[1]
    b = mm(jnp.stack([yre, yim]).reshape(2 * k1 * ch, rows), w2).reshape(2, k1, ch, 2, rows)
    zre = b[0, :, :, 0] - b[1, :, :, 1]
    zim = b[0, :, :, 1] + b[1, :, :, 0]
    ure = zre * tw_c - zim * tw_s
    uim = zre * tw_s + zim * tw_c
    y = mm(wi, jnp.stack([ure, uim]).reshape(2 * k1, ch * rows))
    return y.reshape(blocks, ch, rows)


def body(gate_in, out_gate, value_in, out_grad, skip_gain, filter_taps):
    seq_n = lax.axis_size("seq")
    chan_n = lax.axis_size("chan")
    rows, local_ch = gate_in.shape
    filters = filter_taps.shape[1]
    dev_n = seq_n * chan_n
    per_dev = local_ch // dev_n
    assert local_ch == filters and local_ch % dev_n == 0
    length = 2 * seq_n * rows
    k1 = seq_n + 1

    mixed_bf = lax.optimization_barrier(
        (gate_in.astype(F32) * value_in.astype(F32)).astype(jnp.bfloat16)
    )
    gated_bf = lax.optimization_barrier(
        (out_grad.astype(F32) * out_gate.astype(F32)).astype(jnp.bfloat16)
    )
    mixed = mixed_bf.astype(F32)
    gated = gated_bf.astype(F32)
    skip_grad = lax.psum(jnp.sum(gated * mixed, axis=0), "seq")

    send = jnp.stack(
        [mixed.T.reshape(dev_n, per_dev, rows), gated.T.reshape(dev_n, per_dev, rows)], axis=1
    )
    recv = lax.all_to_all(send, ("seq", "chan"), 0, 0, tiled=True)
    chan_id = lax.axis_index("chan")
    taps_t = filter_taps.T.reshape(seq_n, chan_n, per_dev, rows)
    taps_mine = lax.dynamic_index_in_dim(taps_t, chan_id, axis=1, keepdims=False)
    filt = lax.all_to_all(taps_mine, "seq", 0, 0, tiled=True)

    c1, s1 = trig(k1, seq_n, 2 * seq_n)
    w1 = jnp.concatenate([c1, -s1], axis=0)
    tw_c, tw_s = trig(k1, rows, length)
    tw_c = tw_c[:, None, :]
    tw_s = tw_s[:, None, :]
    c2, s2 = trig(rows, rows, rows)
    w2 = jnp.concatenate([c2, s2], axis=1)
    weight = jnp.where(
        (lax.iota(jnp.int32, k1) == 0) | (lax.iota(jnp.int32, k1) == seq_n), 1.0, 2.0
    ) / length
    ci, si = trig(seq_n, k1, 2 * seq_n)
    wi = jnp.concatenate([ci * weight[None, :], -si * weight[None, :]], axis=1)

    fields = recv.reshape(seq_n, chan_n * 2 * per_dev, rows)
    xre, xim = forward_spectrum(fields, seq_n, rows, w1, tw_c, tw_s, w2)
    xre = xre.reshape(k1, chan_n, 2, per_dev, rows)
    xim = xim.reshape(k1, chan_n, 2, per_dev, rows)
    mre, mim = xre[:, :, 0], xim[:, :, 0]
    gre, gim = xre[:, :, 1], xim[:, :, 1]
    hre, him = forward_spectrum(filt, seq_n, rows, w1, tw_c, tw_s, w2)
    hre = hre[:, None]
    him = him[:, None]

    conv_re = hre * mre - him * mim
    conv_im = hre * mim + him * mre
    corr_re = gre * hre + gim * him
    corr_im = gim * hre - gre * him
    taps_re = jnp.sum(gre * mre + gim * mim, axis=1)
    taps_im = jnp.sum(gim * mre - gre * mim, axis=1)

    yre = jnp.stack([conv_re, corr_re], axis=2).reshape(k1, chan_n * 2 * per_dev, rows)
    yim = jnp.stack([conv_im, corr_im], axis=2).reshape(k1, chan_n * 2 * per_dev, rows)
    y = inverse_real(yre, yim, seq_n, rows, w2, tw_c, tw_s, wi)
    back = lax.all_to_all(y.reshape(dev_n, 2, per_dev, rows), ("seq", "chan"), 0, 0, tiled=True)
    back = back.transpose(1, 0, 2, 3).reshape(2, local_ch, rows)
    conv_out = back[0].T
    corr_out = back[1].T

    taps_pos = inverse_real(taps_re, taps_im, seq_n, rows, w2, tw_c, tw_s, wi)
    taps_blk = lax.all_to_all(taps_pos, "seq", 0, 0, tiled=True)
    taps_all = lax.all_gather(taps_blk, "chan", axis=0, tiled=False)
    taps_grad = taps_all.transpose(1, 0, 2, 3).reshape(filters, rows).T

    out_f32 = out_grad.astype(F32)
    grad_out_gate = (out_f32 * (conv_out + skip_gain[None] * mixed)).astype(jnp.bfloat16)
    mix_grad = corr_out + skip_gain[None] * gated
    grad_gate = (mix_grad * value_in.astype(F32)).astype(jnp.bfloat16)
    grad_value = (mix_grad * gate_in.astype(F32)).astype(jnp.bfloat16)
    return (grad_gate, grad_out_gate, grad_value, skip_grad, taps_grad)


def solution(mesh):
    placed = (
        P("seq", "chan"),
        P("seq", "chan"),
        P("seq", "chan"),
        P("seq", "chan"),
        P("chan"),
        P("seq", None),
    )
    return jax.shard_map(
        body,
        mesh=mesh,
        in_specs=placed,
        out_specs=(P("seq", "chan"), P("seq", "chan"), P("seq", "chan"), P("chan"), P("seq", None)),
        check_vma=False,
    )
```

```python
import math

import jax
import jax.numpy as jnp
from jax import lax
from jax.sharding import PartitionSpec as P

HIGH = lax.Precision.HIGH
F32 = jnp.float32


def trig(a_count, b_count, period, scale=1.0):
    a_ids = lax.iota(jnp.int32, a_count)[:, None]
    b_ids = lax.iota(jnp.int32, b_count)[None, :]
    turns = (a_ids * b_ids) % period
    angle = turns.astype(F32) * (2.0 * math.pi / period)
    return jnp.cos(angle) * scale, jnp.sin(angle) * scale


def mm(a, b):
    return jnp.dot(a, b, precision=HIGH, preferred_element_type=F32)


def forward_spectrum(x, blocks, rows, w1, tw_c, tw_s, w2):
    ch = x.shape[1]
    k1 = blocks + 1
    a = mm(w1, x.reshape(blocks, ch * rows)).reshape(2, k1, ch, rows)
    are, aim = a[0], a[1]
    tre = are * tw_c + aim * tw_s
    tim = aim * tw_c - are * tw_s
    b = mm(jnp.stack([tre, tim]).reshape(2 * k1 * ch, rows), w2).reshape(2, k1, ch, 2, rows)
    xre = b[0, :, :, 0] + b[1, :, :, 1]
    xim = b[1, :, :, 0] - b[0, :, :, 1]
    return xre, xim


def inverse_real(yre, yim, blocks, rows, w2, tw_c, tw_s, wi):
    k1, ch = yre.shape[0], yre.shape[1]
    b = mm(jnp.stack([yre, yim]).reshape(2 * k1 * ch, rows), w2).reshape(2, k1, ch, 2, rows)
    zre = b[0, :, :, 0] - b[1, :, :, 1]
    zim = b[0, :, :, 1] + b[1, :, :, 0]
    ure = zre * tw_c - zim * tw_s
    uim = zre * tw_s + zim * tw_c
    y = mm(wi, jnp.stack([ure, uim]).reshape(2 * k1, ch * rows))
    return y.reshape(blocks, ch, rows)


def body(gate_in, out_gate, value_in, out_grad, skip_gain, filter_taps):
    seq_n = lax.axis_size("seq")
    chan_n = lax.axis_size("chan")
    rows, local_ch = gate_in.shape
    filters = filter_taps.shape[1]
    dev_n = seq_n * chan_n
    per_dev = local_ch // dev_n
    part = rows // chan_n
    assert local_ch == filters and local_ch % dev_n == 0 and rows % chan_n == 0
    length = 2 * seq_n * rows
    k1 = seq_n + 1
    span = per_dev * rows
    pad_w = 128

    mixed_bf = lax.optimization_barrier(
        (gate_in.astype(F32) * value_in.astype(F32)).astype(jnp.bfloat16)
    )
    gated_bf = lax.optimization_barrier(
        (out_grad.astype(F32) * out_gate.astype(F32)).astype(jnp.bfloat16)
    )
    mixed = mixed_bf.astype(F32)
    gated = gated_bf.astype(F32)

    chan_id = lax.axis_index("chan")
    taps_rows = lax.dynamic_slice_in_dim(filter_taps, chan_id * part, part, axis=0)
    send = jnp.concatenate(
        [
            mixed.T.reshape(dev_n, span),
            gated.T.reshape(dev_n, span),
            taps_rows.T.reshape(dev_n, per_dev * part),
        ],
        axis=1,
    )
    recv = lax.all_to_all(send, ("seq", "chan"), 0, 0, tiled=True).reshape(seq_n, chan_n, -1)
    m_pos = recv[:, :, :span].reshape(seq_n, chan_n * per_dev, rows)
    g_pos = recv[:, :, span : 2 * span].reshape(seq_n, chan_n * per_dev, rows)
    h_pos = recv[:, :, 2 * span :].reshape(seq_n, chan_n, per_dev, part)
    h_pos = h_pos.transpose(0, 2, 1, 3).reshape(seq_n, per_dev, rows)
    skip_mine = jnp.sum(m_pos * g_pos, axis=(0, 2)).reshape(chan_n, per_dev)

    c1, s1 = trig(k1, seq_n, 2 * seq_n)
    w1 = jnp.concatenate([c1, -s1], axis=0)
    tw_c, tw_s = trig(k1, rows, length)
    tw_c = tw_c[:, None, :]
    tw_s = tw_s[:, None, :]
    c2, s2 = trig(rows, rows, rows)
    w2 = jnp.concatenate([c2, s2], axis=1)
    weight = jnp.where(
        (lax.iota(jnp.int32, k1) == 0) | (lax.iota(jnp.int32, k1) == seq_n), 1.0, 2.0
    ) / length
    ci, si = trig(seq_n, k1, 2 * seq_n)
    wi = jnp.concatenate([ci * weight[None, :], -si * weight[None, :]], axis=1)

    cc = chan_n * per_dev
    fields = jnp.concatenate([m_pos, g_pos, h_pos], axis=1)
    xre, xim = forward_spectrum(fields, seq_n, rows, w1, tw_c, tw_s, w2)
    mre = xre[:, :cc].reshape(k1, chan_n, per_dev, rows)
    mim = xim[:, :cc].reshape(k1, chan_n, per_dev, rows)
    gre = xre[:, cc : 2 * cc].reshape(k1, chan_n, per_dev, rows)
    gim = xim[:, cc : 2 * cc].reshape(k1, chan_n, per_dev, rows)
    hre = xre[:, 2 * cc :][:, None]
    him = xim[:, 2 * cc :][:, None]

    conv_re = hre * mre - him * mim
    conv_im = hre * mim + him * mre
    corr_re = gre * hre + gim * him
    corr_im = gim * hre - gre * him
    taps_re = jnp.sum(gre * mre + gim * mim, axis=1)
    taps_im = jnp.sum(gim * mre - gre * mim, axis=1)

    yre = jnp.concatenate(
        [conv_re.reshape(k1, cc, rows), corr_re.reshape(k1, cc, rows), taps_re], axis=1
    )
    yim = jnp.concatenate(
        [conv_im.reshape(k1, cc, rows), corr_im.reshape(k1, cc, rows), taps_im], axis=1
    )
    y = inverse_real(yre, yim, seq_n, rows, w2, tw_c, tw_s, wi)
    conv_blk = y[:, :cc].reshape(seq_n, chan_n, span)
    corr_blk = y[:, cc : 2 * cc].reshape(seq_n, chan_n, span)
    taps_blk = jnp.broadcast_to(y[:, 2 * cc :].reshape(seq_n, 1, span), (seq_n, chan_n, span))
    skip_blk = jnp.broadcast_to(
        jnp.pad(skip_mine, ((0, 0), (0, pad_w - per_dev)))[None], (seq_n, chan_n, pad_w)
    )
    out_send = jnp.concatenate([conv_blk, corr_blk, taps_blk, skip_blk], axis=2)
    back = lax.all_to_all(out_send.reshape(dev_n, -1), ("seq", "chan"), 0, 0, tiled=True)
    conv_out = back[:, :span].reshape(local_ch, rows).T
    corr_out = back[:, span : 2 * span].reshape(local_ch, rows).T
    taps_grad = back[:, 2 * span : 3 * span].reshape(filters, rows).T
    skip_grad = back[:, 3 * span : 3 * span + per_dev].reshape(local_ch)

    out_f32 = out_grad.astype(F32)
    grad_out_gate = (out_f32 * (conv_out + skip_gain[None] * mixed)).astype(jnp.bfloat16)
    mix_grad = corr_out + skip_gain[None] * gated
    grad_gate = (mix_grad * value_in.astype(F32)).astype(jnp.bfloat16)
    grad_value = (mix_grad * gate_in.astype(F32)).astype(jnp.bfloat16)
    return (grad_gate, grad_out_gate, grad_value, skip_grad, taps_grad)


def solution(mesh):
    placed = (
        P("seq", "chan"),
        P("seq", "chan"),
        P("seq", "chan"),
        P("seq", "chan"),
        P("chan"),
        P("seq", None),
    )
    return jax.shard_map(
        body,
        mesh=mesh,
        in_specs=placed,
        out_specs=(P("seq", "chan"), P("seq", "chan"), P("seq", "chan"), P("chan"), P("seq", None)),
        check_vma=False,
    )
```

```python
import math

import jax
import jax.numpy as jnp
from jax import lax
from jax.sharding import PartitionSpec as P

HIGH = lax.Precision.HIGH
F32 = jnp.float32


def trig(a_count, b_count, period, scale=1.0):
    a_ids = lax.iota(jnp.int32, a_count)[:, None]
    b_ids = lax.iota(jnp.int32, b_count)[None, :]
    turns = (a_ids * b_ids) % period
    angle = turns.astype(F32) * (2.0 * math.pi / period)
    return jnp.cos(angle) * scale, jnp.sin(angle) * scale


def mm(spec, a, b):
    return jnp.einsum(spec, a, b, precision=HIGH, preferred_element_type=F32)


def body(gate_in, out_gate, value_in, out_grad, skip_gain, filter_taps):
    seq_n = lax.axis_size("seq")
    chan_n = lax.axis_size("chan")
    rows, local_ch = gate_in.shape
    filters = filter_taps.shape[1]
    dev_n = seq_n * chan_n
    per_dev = local_ch // dev_n
    part = rows // chan_n
    assert local_ch == filters and local_ch % dev_n == 0 and rows % chan_n == 0
    length = 2 * seq_n * rows
    k1 = seq_n + 1
    span = per_dev * rows
    cc = chan_n * per_dev
    pad_w = 128

    mixed_bf = lax.optimization_barrier(
        (gate_in.astype(F32) * value_in.astype(F32)).astype(jnp.bfloat16)
    )
    gated_bf = lax.optimization_barrier(
        (out_grad.astype(F32) * out_gate.astype(F32)).astype(jnp.bfloat16)
    )
    mixed = mixed_bf.astype(F32)
    gated = gated_bf.astype(F32)

    chan_id = lax.axis_index("chan")
    taps_rows = lax.dynamic_slice_in_dim(filter_taps, chan_id * part, part, axis=0)
    send = jnp.concatenate(
        [
            mixed.T.reshape(dev_n, span),
            gated.T.reshape(dev_n, span),
            taps_rows.T.reshape(dev_n, per_dev * part),
        ],
        axis=1,
    )
    recv = lax.all_to_all(send, ("seq", "chan"), 0, 0, tiled=True).reshape(seq_n, chan_n, -1)

    def by_filter(block):
        return block.reshape(seq_n, chan_n, per_dev, rows).transpose(0, 2, 1, 3).reshape(seq_n, cc, rows)

    m_pos = by_filter(recv[:, :, :span])
    g_pos = by_filter(recv[:, :, span : 2 * span])
    h_pos = recv[:, :, 2 * span :].reshape(seq_n, chan_n, per_dev, part)
    h_pos = h_pos.transpose(0, 2, 1, 3).reshape(seq_n, per_dev, rows)
    skip_mine = jnp.sum(m_pos * g_pos, axis=(0, 2)).reshape(per_dev, chan_n).T

    c1, s1 = trig(k1, seq_n, 2 * seq_n)
    tw_c, tw_s = trig(k1, rows, length)
    tw_c = tw_c[:, None, :]
    tw_s = tw_s[:, None, :]
    c2, s2 = trig(rows, rows, rows)
    w_fwd = jnp.concatenate(
        [jnp.concatenate([c2, -s2], axis=1), jnp.concatenate([s2, c2], axis=1)], axis=0
    )
    w_inv = jnp.concatenate(
        [jnp.concatenate([c2, s2], axis=1), jnp.concatenate([-s2, c2], axis=1)], axis=0
    )
    weight = jnp.where(
        (lax.iota(jnp.int32, k1) == 0) | (lax.iota(jnp.int32, k1) == seq_n), 1.0, 2.0
    ) / length
    ci, si = trig(seq_n, k1, 2 * seq_n)
    ci = ci * weight[None, :]
    si = si * weight[None, :]

    fields = jnp.concatenate([m_pos, g_pos, h_pos], axis=1)
    are = mm("ks,scr->kcr", c1, fields)
    aim = mm("ks,scr->kcr", -s1, fields)
    turned = jnp.concatenate([are * tw_c + aim * tw_s, aim * tw_c - are * tw_s], axis=2)
    spec = mm("kcn,nm->kcm", turned, w_fwd)

    mre, mim = spec[:, :cc, :rows], spec[:, :cc, rows:]
    gre, gim = spec[:, cc : 2 * cc, :rows], spec[:, cc : 2 * cc, rows:]
    h = spec[:, 2 * cc :]
    h = jnp.broadcast_to(h[:, :, None, :], (k1, per_dev, chan_n, 2 * rows)).reshape(k1, cc, 2 * rows)
    hre, him = h[:, :, :rows], h[:, :, rows:]

    conv_s = jnp.concatenate([hre * mre - him * mim, hre * mim + him * mre], axis=2)
    corr_s = jnp.concatenate([gre * hre + gim * him, gim * hre - gre * him], axis=2)
    taps_s = jnp.concatenate([gre * mre + gim * mim, gim * mre - gre * mim], axis=2)
    taps_s = jnp.sum(taps_s.reshape(k1, per_dev, chan_n, 2 * rows), axis=2)

    prod = jnp.concatenate([conv_s, corr_s, taps_s], axis=1)
    z = mm("kcn,nm->kcm", prod, w_inv)
    zre, zim = z[:, :, :rows], z[:, :, rows:]
    ure = zre * tw_c - zim * tw_s
    uim = zre * tw_s + zim * tw_c
    y = mm("ik,kcr->icr", ci, ure) - mm("ik,kcr->icr", si, uim)

    def by_copy(block):
        return block.reshape(seq_n, per_dev, chan_n, rows).transpose(0, 2, 1, 3).reshape(seq_n, chan_n, span)

    conv_blk = by_copy(y[:, :cc])
    corr_blk = by_copy(y[:, cc : 2 * cc])
    taps_blk = jnp.broadcast_to(y[:, 2 * cc :].reshape(seq_n, 1, span), (seq_n, chan_n, span))
    skip_blk = jnp.broadcast_to(
        jnp.pad(skip_mine, ((0, 0), (0, pad_w - per_dev)))[None], (seq_n, chan_n, pad_w)
    )
    out_send = jnp.concatenate([conv_blk, corr_blk, taps_blk, skip_blk], axis=2)
    back = lax.all_to_all(out_send.reshape(dev_n, -1), ("seq", "chan"), 0, 0, tiled=True)
    conv_out = back[:, :span].reshape(local_ch, rows).T
    corr_out = back[:, span : 2 * span].reshape(local_ch, rows).T
    taps_grad = back[:, 2 * span : 3 * span].reshape(filters, rows).T
    skip_grad = back[:, 3 * span : 3 * span + per_dev].reshape(local_ch)

    out_f32 = out_grad.astype(F32)
    grad_out_gate = (out_f32 * (conv_out + skip_gain[None] * mixed)).astype(jnp.bfloat16)
    mix_grad = corr_out + skip_gain[None] * gated
    grad_gate = (mix_grad * value_in.astype(F32)).astype(jnp.bfloat16)
    grad_value = (mix_grad * gate_in.astype(F32)).astype(jnp.bfloat16)
    return (grad_gate, grad_out_gate, grad_value, skip_grad, taps_grad)


def solution(mesh):
    placed = (
        P("seq", "chan"),
        P("seq", "chan"),
        P("seq", "chan"),
        P("seq", "chan"),
        P("chan"),
        P("seq", None),
    )
    return jax.shard_map(
        body,
        mesh=mesh,
        in_specs=placed,
        out_specs=(P("seq", "chan"), P("seq", "chan"), P("seq", "chan"), P("chan"), P("seq", None)),
        check_vma=False,
    )
```

```python
import math

import jax
import jax.numpy as jnp
from jax import lax
from jax.sharding import PartitionSpec as P

HIGH = lax.Precision.HIGH
F32 = jnp.float32


def trig(a_count, b_count, period, scale=1.0):
    a_ids = lax.iota(jnp.int32, a_count)[:, None]
    b_ids = lax.iota(jnp.int32, b_count)[None, :]
    turns = (a_ids * b_ids) % period
    angle = turns.astype(F32) * (2.0 * math.pi / period)
    return jnp.cos(angle) * scale, jnp.sin(angle) * scale


def mm(spec, a, b):
    return jnp.einsum(spec, a, b, precision=HIGH, preferred_element_type=F32)


def body(gate_in, out_gate, value_in, out_grad, skip_gain, filter_taps):
    seq_n = lax.axis_size("seq")
    chan_n = lax.axis_size("chan")
    rows, local_ch = gate_in.shape
    filters = filter_taps.shape[1]
    dev_n = seq_n * chan_n
    per_dev = local_ch // dev_n
    part = rows // chan_n
    assert local_ch == filters and local_ch % dev_n == 0 and rows % chan_n == 0
    length = 2 * seq_n * rows
    k1 = seq_n + 1
    span = per_dev * rows
    cc = chan_n * per_dev
    pad_w = 128

    mixed_bf = lax.optimization_barrier(
        (gate_in.astype(F32) * value_in.astype(F32)).astype(jnp.bfloat16)
    )
    gated_bf = lax.optimization_barrier(
        (out_grad.astype(F32) * out_gate.astype(F32)).astype(jnp.bfloat16)
    )
    mixed = mixed_bf.astype(F32)
    gated = gated_bf.astype(F32)

    chan_id = lax.axis_index("chan")
    taps_rows = lax.dynamic_slice_in_dim(filter_taps, chan_id * part, part, axis=0)
    def by_target(block):
        width = block.shape[0]
        return block.T.reshape(per_dev, dev_n, width).transpose(1, 0, 2).reshape(dev_n, per_dev * width)

    send = jnp.concatenate([by_target(mixed), by_target(gated), by_target(taps_rows)], axis=1)
    recv = lax.all_to_all(send, ("seq", "chan"), 0, 0, tiled=True).reshape(seq_n, chan_n, -1)

    def by_filter(block):
        return block.reshape(seq_n, chan_n, per_dev, rows).transpose(0, 2, 1, 3).reshape(seq_n, cc, rows)

    m_pos = by_filter(recv[:, :, :span])
    g_pos = by_filter(recv[:, :, span : 2 * span])
    h_pos = recv[:, :, 2 * span :].reshape(seq_n, chan_n, per_dev, part)
    h_pos = h_pos.transpose(0, 2, 1, 3).reshape(seq_n, per_dev, rows)
    skip_mine = jnp.sum(m_pos * g_pos, axis=(0, 2)).reshape(per_dev, chan_n).T

    c1, s1 = trig(k1, seq_n, 2 * seq_n)
    tw_c, tw_s = trig(k1, rows, length)
    tw_c = tw_c[:, None, :]
    tw_s = tw_s[:, None, :]
    c2, s2 = trig(rows, rows, rows)
    w_fwd = jnp.concatenate(
        [jnp.concatenate([c2, -s2], axis=1), jnp.concatenate([s2, c2], axis=1)], axis=0
    )
    w_inv = jnp.concatenate(
        [jnp.concatenate([c2, s2], axis=1), jnp.concatenate([-s2, c2], axis=1)], axis=0
    )
    weight = jnp.where(
        (lax.iota(jnp.int32, k1) == 0) | (lax.iota(jnp.int32, k1) == seq_n), 1.0, 2.0
    ) / length
    ci, si = trig(seq_n, k1, 2 * seq_n)
    ci = ci * weight[None, :]
    si = si * weight[None, :]

    fields = jnp.concatenate([m_pos, g_pos, h_pos], axis=1)
    are = mm("ks,scr->kcr", c1, fields)
    aim = mm("ks,scr->kcr", -s1, fields)
    turned = jnp.concatenate([are * tw_c + aim * tw_s, aim * tw_c - are * tw_s], axis=2)
    spec = mm("kcn,nm->kcm", turned, w_fwd)

    mre, mim = spec[:, :cc, :rows], spec[:, :cc, rows:]
    gre, gim = spec[:, cc : 2 * cc, :rows], spec[:, cc : 2 * cc, rows:]
    h = spec[:, 2 * cc :]
    h = jnp.broadcast_to(h[:, :, None, :], (k1, per_dev, chan_n, 2 * rows)).reshape(k1, cc, 2 * rows)
    hre, him = h[:, :, :rows], h[:, :, rows:]

    conv_s = jnp.concatenate([hre * mre - him * mim, hre * mim + him * mre], axis=2)
    corr_s = jnp.concatenate([gre * hre + gim * him, gim * hre - gre * him], axis=2)
    taps_s = jnp.concatenate([gre * mre + gim * mim, gim * mre - gre * mim], axis=2)
    taps_s = jnp.sum(taps_s.reshape(k1, per_dev, chan_n, 2 * rows), axis=2)

    prod = jnp.concatenate([conv_s, corr_s, taps_s], axis=1)
    z = mm("kcn,nm->kcm", prod, w_inv)
    zre, zim = z[:, :, :rows], z[:, :, rows:]
    ure = zre * tw_c - zim * tw_s
    uim = zre * tw_s + zim * tw_c
    y = mm("ik,kcr->icr", ci, ure) - mm("ik,kcr->icr", si, uim)

    def by_copy(block):
        return block.reshape(seq_n, per_dev, chan_n, rows).transpose(0, 2, 1, 3).reshape(seq_n, chan_n, span)

    conv_blk = by_copy(y[:, :cc])
    corr_blk = by_copy(y[:, cc : 2 * cc])
    taps_blk = jnp.broadcast_to(y[:, 2 * cc :].reshape(seq_n, 1, span), (seq_n, chan_n, span))
    skip_blk = jnp.broadcast_to(
        jnp.pad(skip_mine, ((0, 0), (0, pad_w - per_dev)))[None], (seq_n, chan_n, pad_w)
    )
    out_send = jnp.concatenate([conv_blk, corr_blk, taps_blk, skip_blk], axis=2)
    back = lax.all_to_all(out_send.reshape(dev_n, -1), ("seq", "chan"), 0, 0, tiled=True)
    def by_channel(start):
        return jnp.concatenate(
            [back[:, start + f2 * rows : start + (f2 + 1) * rows].T for f2 in range(per_dev)], axis=1
        )

    conv_out = by_channel(0)
    corr_out = by_channel(span)
    taps_grad = by_channel(2 * span)
    skip_grad = back[:, 3 * span : 3 * span + per_dev].T.reshape(local_ch)

    out_f32 = out_grad.astype(F32)
    grad_out_gate = (out_f32 * (conv_out + skip_gain[None] * mixed)).astype(jnp.bfloat16)
    mix_grad = corr_out + skip_gain[None] * gated
    grad_gate = (mix_grad * value_in.astype(F32)).astype(jnp.bfloat16)
    grad_value = (mix_grad * gate_in.astype(F32)).astype(jnp.bfloat16)
    return (grad_gate, grad_out_gate, grad_value, skip_grad, taps_grad)


def solution(mesh):
    placed = (
        P("seq", "chan"),
        P("seq", "chan"),
        P("seq", "chan"),
        P("seq", "chan"),
        P("chan"),
        P("seq", None),
    )
    return jax.shard_map(
        body,
        mesh=mesh,
        in_specs=placed,
        out_specs=(P("seq", "chan"), P("seq", "chan"), P("seq", "chan"), P("chan"), P("seq", None)),
        check_vma=False,
    )
```

```python
import math

import jax
import jax.numpy as jnp
from jax import lax
from jax.experimental import pallas as pl
from jax.experimental.pallas import tpu as pltpu
from jax.sharding import PartitionSpec as P

HIGH = lax.Precision.HIGH
F32 = jnp.float32


def trig(a_count, b_count, period, scale=1.0):
    a_ids = lax.iota(jnp.int32, a_count)[:, None]
    b_ids = lax.iota(jnp.int32, b_count)[None, :]
    turns = (a_ids * b_ids) % period
    angle = turns.astype(F32) * (2.0 * math.pi / period)
    return jnp.cos(angle) * scale, jnp.sin(angle) * scale


def mm(spec, a, b):
    return jnp.einsum(spec, a, b, precision=HIGH, preferred_element_type=F32)


def body(gate_in, out_gate, value_in, out_grad, skip_gain, filter_taps):
    seq_n = lax.axis_size("seq")
    chan_n = lax.axis_size("chan")
    rows, local_ch = gate_in.shape
    filters = filter_taps.shape[1]
    dev_n = seq_n * chan_n
    per_dev = local_ch // dev_n
    part = rows // chan_n
    assert local_ch == filters and local_ch % dev_n == 0 and rows % chan_n == 0
    length = 2 * seq_n * rows
    k1 = seq_n + 1
    span = per_dev * rows
    cc = chan_n * per_dev
    pad_w = 128

    chan_id = lax.axis_index("chan")
    taps_rows = lax.dynamic_slice_in_dim(filter_taps, chan_id * part, part, axis=0)
    taps_send = taps_rows.T.reshape(per_dev, dev_n, part).transpose(1, 0, 2).reshape(dev_n, per_dev * part)

    def prep_kernel(gi, vi, og, ot, tr, send):
        for f2 in range(per_dev):
            lanes = pl.ds(f2 * dev_n, dev_n)
            m = (gi[:, lanes].astype(F32) * vi[:, lanes].astype(F32)).astype(jnp.bfloat16).astype(F32)
            g = (og[:, lanes].astype(F32) * ot[:, lanes].astype(F32)).astype(jnp.bfloat16).astype(F32)
            send[:, pl.ds(f2 * rows, rows)] = m.T
            send[:, pl.ds(span + f2 * rows, rows)] = g.T
        send[:, pl.ds(2 * span, per_dev * part)] = tr[...]

    send = pl.pallas_call(
        prep_kernel,
        out_shape=jax.ShapeDtypeStruct((dev_n, 2 * span + per_dev * part), F32),
        cost_estimate=pl.CostEstimate(flops=4 * rows * local_ch, transcendentals=0, bytes_accessed=4 * 2 * rows * local_ch * 2),
    )(gate_in, value_in, out_grad, out_gate, taps_send)
    recv = lax.all_to_all(send, ("seq", "chan"), 0, 0, tiled=True).reshape(seq_n, chan_n, -1)

    def by_filter(block):
        return block.reshape(seq_n, chan_n, per_dev, rows).transpose(0, 2, 1, 3).reshape(seq_n, cc, rows)

    m_pos = by_filter(recv[:, :, :span])
    g_pos = by_filter(recv[:, :, span : 2 * span])
    h_pos = recv[:, :, 2 * span :].reshape(seq_n, chan_n, per_dev, part)
    h_pos = h_pos.transpose(0, 2, 1, 3).reshape(seq_n, per_dev, rows)
    skip_mine = jnp.sum(m_pos * g_pos, axis=(0, 2)).reshape(per_dev, chan_n).T

    c1, s1 = trig(k1, seq_n, 2 * seq_n)
    tw_c, tw_s = trig(k1, rows, length)
    tw_c = tw_c[:, None, :]
    tw_s = tw_s[:, None, :]
    c2, s2 = trig(rows, rows, rows)
    w_fwd = jnp.concatenate(
        [jnp.concatenate([c2, -s2], axis=1), jnp.concatenate([s2, c2], axis=1)], axis=0
    )
    w_inv = jnp.concatenate(
        [jnp.concatenate([c2, s2], axis=1), jnp.concatenate([-s2, c2], axis=1)], axis=0
    )
    weight = jnp.where(
        (lax.iota(jnp.int32, k1) == 0) | (lax.iota(jnp.int32, k1) == seq_n), 1.0, 2.0
    ) / length
    ci, si = trig(seq_n, k1, 2 * seq_n)
    ci = ci * weight[None, :]
    si = si * weight[None, :]

    fields = jnp.concatenate([m_pos, g_pos, h_pos], axis=1)
    are = mm("ks,scr->kcr", c1, fields)
    aim = mm("ks,scr->kcr", -s1, fields)
    turned = jnp.concatenate([are * tw_c + aim * tw_s, aim * tw_c - are * tw_s], axis=2)
    spec = mm("kcn,nm->kcm", turned, w_fwd)

    mre, mim = spec[:, :cc, :rows], spec[:, :cc, rows:]
    gre, gim = spec[:, cc : 2 * cc, :rows], spec[:, cc : 2 * cc, rows:]
    h = spec[:, 2 * cc :]
    h = jnp.broadcast_to(h[:, :, None, :], (k1, per_dev, chan_n, 2 * rows)).reshape(k1, cc, 2 * rows)
    hre, him = h[:, :, :rows], h[:, :, rows:]

    conv_s = jnp.concatenate([hre * mre - him * mim, hre * mim + him * mre], axis=2)
    corr_s = jnp.concatenate([gre * hre + gim * him, gim * hre - gre * him], axis=2)
    taps_s = jnp.concatenate([gre * mre + gim * mim, gim * mre - gre * mim], axis=2)
    taps_s = jnp.sum(taps_s.reshape(k1, per_dev, chan_n, 2 * rows), axis=2)

    prod = jnp.concatenate([conv_s, corr_s, taps_s], axis=1)
    z = mm("kcn,nm->kcm", prod, w_inv)
    zre, zim = z[:, :, :rows], z[:, :, rows:]
    ure = zre * tw_c - zim * tw_s
    uim = zre * tw_s + zim * tw_c
    y = mm("ik,kcr->icr", ci, ure) - mm("ik,kcr->icr", si, uim)

    def by_copy(block):
        return block.reshape(seq_n, per_dev, chan_n, rows).transpose(0, 2, 1, 3).reshape(seq_n, chan_n, span)

    conv_blk = by_copy(y[:, :cc])
    corr_blk = by_copy(y[:, cc : 2 * cc])
    taps_blk = jnp.broadcast_to(y[:, 2 * cc :].reshape(seq_n, 1, span), (seq_n, chan_n, span))
    skip_blk = jnp.broadcast_to(
        jnp.pad(skip_mine, ((0, 0), (0, pad_w - per_dev)))[None], (seq_n, chan_n, pad_w)
    )
    out_send = jnp.concatenate([conv_blk, corr_blk, taps_blk, skip_blk], axis=2)
    back = lax.all_to_all(out_send.reshape(dev_n, -1), ("seq", "chan"), 0, 0, tiled=True)
    def tail_kernel(bk, gi, vi, og, ot, sg, o_gg, o_gog, o_gv, o_taps, o_skip):
        for f2 in range(per_dev):
            lanes = pl.ds(f2 * dev_n, dev_n)
            conv = bk[:, pl.ds(f2 * rows, rows)].T
            corr = bk[:, pl.ds(span + f2 * rows, rows)].T
            o_taps[:, lanes] = bk[:, pl.ds(2 * span + f2 * rows, rows)].T
            gate = gi[:, lanes].astype(F32)
            val = vi[:, lanes].astype(F32)
            outg = og[:, lanes].astype(F32)
            m = (gate * val).astype(jnp.bfloat16).astype(F32)
            g = (outg * ot[:, lanes].astype(F32)).astype(jnp.bfloat16).astype(F32)
            s = sg[:, lanes]
            o_gog[:, lanes] = (outg * (conv + s * m)).astype(jnp.bfloat16)
            mix = corr + s * g
            o_gg[:, lanes] = (mix * val).astype(jnp.bfloat16)
            o_gv[:, lanes] = (mix * gate).astype(jnp.bfloat16)
        o_skip[...] = bk[:, pl.ds(3 * span, pad_w)].T[:per_dev, :]

    grad_shape = jax.ShapeDtypeStruct((rows, local_ch), jnp.bfloat16)
    grad_gate, grad_out_gate, grad_value, taps_grad, skip_two = pl.pallas_call(
        tail_kernel,
        out_shape=(
            grad_shape,
            grad_shape,
            grad_shape,
            jax.ShapeDtypeStruct((rows, filters), F32),
            jax.ShapeDtypeStruct((per_dev, dev_n), F32),
        ),
        cost_estimate=pl.CostEstimate(flops=12 * rows * local_ch, transcendentals=0, bytes_accessed=4 * 4 * rows * local_ch * 2),
    )(back, gate_in, value_in, out_grad, out_gate, skip_gain.reshape(1, local_ch))
    skip_grad = skip_two.reshape(local_ch)
    return (grad_gate, grad_out_gate, grad_value, skip_grad, taps_grad)


def solution(mesh):
    placed = (
        P("seq", "chan"),
        P("seq", "chan"),
        P("seq", "chan"),
        P("seq", "chan"),
        P("chan"),
        P("seq", None),
    )
    return jax.shard_map(
        body,
        mesh=mesh,
        in_specs=placed,
        out_specs=(P("seq", "chan"), P("seq", "chan"), P("seq", "chan"), P("chan"), P("seq", None)),
        check_vma=False,
    )
```

```python
import math

import jax
import jax.numpy as jnp
from jax import lax
from jax.experimental import pallas as pl
from jax.experimental.pallas import tpu as pltpu
from jax.sharding import PartitionSpec as P

HIGH = lax.Precision.HIGH
F32 = jnp.float32


def trig(a_count, b_count, period, scale=1.0):
    a_ids = lax.iota(jnp.int32, a_count)[:, None]
    b_ids = lax.iota(jnp.int32, b_count)[None, :]
    turns = (a_ids * b_ids) % period
    angle = turns.astype(F32) * (2.0 * math.pi / period)
    return jnp.cos(angle) * scale, jnp.sin(angle) * scale


def mm(spec, a, b):
    return jnp.einsum(spec, a, b, precision=HIGH, preferred_element_type=F32)


def body(gate_in, out_gate, value_in, out_grad, skip_gain, filter_taps):
    seq_n = lax.axis_size("seq")
    chan_n = lax.axis_size("chan")
    rows, local_ch = gate_in.shape
    filters = filter_taps.shape[1]
    dev_n = seq_n * chan_n
    per_dev = local_ch // dev_n
    part = rows // chan_n
    assert local_ch == filters and local_ch % dev_n == 0 and rows % chan_n == 0
    length = 2 * seq_n * rows
    k1 = seq_n + 1
    span = per_dev * rows
    cc = chan_n * per_dev
    pad_w = 128

    chan_id = lax.axis_index("chan")
    taps_rows = lax.dynamic_slice_in_dim(filter_taps, chan_id * part, part, axis=0)
    taps_send = taps_rows.T.reshape(per_dev, dev_n, part).transpose(1, 0, 2).reshape(dev_n, per_dev * part)

    lane = 128
    send_w = (2 * span + per_dev * part) // lane
    back_w = (3 * span + pad_w) // lane
    rq = rows // lane

    def prep_kernel(gi, vi, og, ot, tr, send):
        for f2 in range(per_dev):
            lanes = pl.ds(f2 * dev_n, dev_n)
            m = (gi[:, lanes].astype(F32) * vi[:, lanes].astype(F32)).astype(jnp.bfloat16).astype(F32).T
            g = (og[:, lanes].astype(F32) * ot[:, lanes].astype(F32)).astype(jnp.bfloat16).astype(F32).T
            for q in range(rq):
                send[pl.ds(f2 * rq + q, dev_n, stride=send_w), :] = m[:, q * lane : (q + 1) * lane]
                send[pl.ds((per_dev + f2) * rq + q, dev_n, stride=send_w), :] = g[:, q * lane : (q + 1) * lane]
        send[pl.ds(2 * per_dev * rq, dev_n, stride=send_w), :] = tr[...]

    send = pl.pallas_call(
        prep_kernel,
        out_shape=jax.ShapeDtypeStruct((dev_n * send_w, lane), F32),
        cost_estimate=pl.CostEstimate(flops=4 * rows * local_ch, transcendentals=0, bytes_accessed=4 * 2 * rows * local_ch * 2),
    )(gate_in, value_in, out_grad, out_gate, taps_send).reshape(dev_n, send_w * lane)
    recv = lax.all_to_all(send, ("seq", "chan"), 0, 0, tiled=True).reshape(seq_n, chan_n, -1)

    def by_filter(block):
        return block.reshape(seq_n, chan_n, per_dev, rows).transpose(0, 2, 1, 3).reshape(seq_n, cc, rows)

    m_pos = by_filter(recv[:, :, :span])
    g_pos = by_filter(recv[:, :, span : 2 * span])
    h_pos = recv[:, :, 2 * span :].reshape(seq_n, chan_n, per_dev, part)
    h_pos = h_pos.transpose(0, 2, 1, 3).reshape(seq_n, per_dev, rows)
    skip_mine = jnp.sum(m_pos * g_pos, axis=(0, 2)).reshape(per_dev, chan_n).T

    c1, s1 = trig(k1, seq_n, 2 * seq_n)
    tw_c, tw_s = trig(k1, rows, length)
    tw_c = tw_c[:, None, :]
    tw_s = tw_s[:, None, :]
    c2, s2 = trig(rows, rows, rows)
    w_fwd = jnp.concatenate(
        [jnp.concatenate([c2, -s2], axis=1), jnp.concatenate([s2, c2], axis=1)], axis=0
    )
    w_inv = jnp.concatenate(
        [jnp.concatenate([c2, s2], axis=1), jnp.concatenate([-s2, c2], axis=1)], axis=0
    )
    weight = jnp.where(
        (lax.iota(jnp.int32, k1) == 0) | (lax.iota(jnp.int32, k1) == seq_n), 1.0, 2.0
    ) / length
    ci, si = trig(seq_n, k1, 2 * seq_n)
    ci = ci * weight[None, :]
    si = si * weight[None, :]

    fields = jnp.concatenate([m_pos, g_pos, h_pos], axis=1)
    are = mm("ks,scr->kcr", c1, fields)
    aim = mm("ks,scr->kcr", -s1, fields)
    turned = jnp.concatenate([are * tw_c + aim * tw_s, aim * tw_c - are * tw_s], axis=2)
    spec = mm("kcn,nm->kcm", turned, w_fwd)

    mre, mim = spec[:, :cc, :rows], spec[:, :cc, rows:]
    gre, gim = spec[:, cc : 2 * cc, :rows], spec[:, cc : 2 * cc, rows:]
    h = spec[:, 2 * cc :]
    h = jnp.broadcast_to(h[:, :, None, :], (k1, per_dev, chan_n, 2 * rows)).reshape(k1, cc, 2 * rows)
    hre, him = h[:, :, :rows], h[:, :, rows:]

    conv_s = jnp.concatenate([hre * mre - him * mim, hre * mim + him * mre], axis=2)
    corr_s = jnp.concatenate([gre * hre + gim * him, gim * hre - gre * him], axis=2)
    taps_s = jnp.concatenate([gre * mre + gim * mim, gim * mre - gre * mim], axis=2)
    taps_s = jnp.sum(taps_s.reshape(k1, per_dev, chan_n, 2 * rows), axis=2)

    prod = jnp.concatenate([conv_s, corr_s, taps_s], axis=1)
    z = mm("kcn,nm->kcm", prod, w_inv)
    zre, zim = z[:, :, :rows], z[:, :, rows:]
    ure = zre * tw_c - zim * tw_s
    uim = zre * tw_s + zim * tw_c
    y = mm("ik,kcr->icr", ci, ure) - mm("ik,kcr->icr", si, uim)

    def by_copy(block):
        return block.reshape(seq_n, per_dev, chan_n, rows).transpose(0, 2, 1, 3).reshape(seq_n, chan_n, span)

    conv_blk = by_copy(y[:, :cc])
    corr_blk = by_copy(y[:, cc : 2 * cc])
    taps_blk = jnp.broadcast_to(y[:, 2 * cc :].reshape(seq_n, 1, span), (seq_n, chan_n, span))
    skip_blk = jnp.broadcast_to(
        jnp.pad(skip_mine, ((0, 0), (0, pad_w - per_dev)))[None], (seq_n, chan_n, pad_w)
    )
    out_send = jnp.concatenate([conv_blk, corr_blk, taps_blk, skip_blk], axis=2)
    back = lax.all_to_all(out_send.reshape(dev_n, -1), ("seq", "chan"), 0, 0, tiled=True)
    def tail_kernel(bk, gi, vi, og, ot, sg, o_gg, o_gog, o_gv, o_taps, o_skip):
        def field(first):
            parts = [bk[pl.ds(first + q, dev_n, stride=back_w), :] for q in range(rq)]
            return jnp.concatenate(parts, axis=1).T

        for f2 in range(per_dev):
            lanes = pl.ds(f2 * dev_n, dev_n)
            conv = field(f2 * rq)
            corr = field((per_dev + f2) * rq)
            o_taps[:, lanes] = field((2 * per_dev + f2) * rq)
            gate = gi[:, lanes].astype(F32)
            val = vi[:, lanes].astype(F32)
            outg = og[:, lanes].astype(F32)
            m = (gate * val).astype(jnp.bfloat16).astype(F32)
            g = (outg * ot[:, lanes].astype(F32)).astype(jnp.bfloat16).astype(F32)
            s = sg[:, lanes]
            o_gog[:, lanes] = (outg * (conv + s * m)).astype(jnp.bfloat16)
            mix = corr + s * g
            o_gg[:, lanes] = (mix * val).astype(jnp.bfloat16)
            o_gv[:, lanes] = (mix * gate).astype(jnp.bfloat16)
        o_skip[...] = bk[pl.ds(3 * per_dev * rq, dev_n, stride=back_w), :].T[:per_dev, :]

    grad_shape = jax.ShapeDtypeStruct((rows, local_ch), jnp.bfloat16)
    grad_gate, grad_out_gate, grad_value, taps_grad, skip_two = pl.pallas_call(
        tail_kernel,
        out_shape=(
            grad_shape,
            grad_shape,
            grad_shape,
            jax.ShapeDtypeStruct((rows, filters), F32),
            jax.ShapeDtypeStruct((per_dev, dev_n), F32),
        ),
        cost_estimate=pl.CostEstimate(flops=12 * rows * local_ch, transcendentals=0, bytes_accessed=4 * 4 * rows * local_ch * 2),
    )(back.reshape(dev_n * back_w, lane), gate_in, value_in, out_grad, out_gate, skip_gain.reshape(1, local_ch))
    skip_grad = skip_two.reshape(local_ch)
    return (grad_gate, grad_out_gate, grad_value, skip_grad, taps_grad)


def solution(mesh):
    placed = (
        P("seq", "chan"),
        P("seq", "chan"),
        P("seq", "chan"),
        P("seq", "chan"),
        P("chan"),
        P("seq", None),
    )
    return jax.shard_map(
        body,
        mesh=mesh,
        in_specs=placed,
        out_specs=(P("seq", "chan"), P("seq", "chan"), P("seq", "chan"), P("chan"), P("seq", None)),
        check_vma=False,
    )
```

```python
import math

import jax
import jax.numpy as jnp
from jax import lax
from jax.experimental import pallas as pl
from jax.experimental.pallas import tpu as pltpu
from jax.sharding import PartitionSpec as P

HIGH = lax.Precision.HIGH
F32 = jnp.float32


def trig(a_count, b_count, period, scale=1.0):
    a_ids = lax.iota(jnp.int32, a_count)[:, None]
    b_ids = lax.iota(jnp.int32, b_count)[None, :]
    turns = (a_ids * b_ids) % period
    angle = turns.astype(F32) * (2.0 * math.pi / period)
    return jnp.cos(angle) * scale, jnp.sin(angle) * scale


def mm(spec, a, b):
    return jnp.einsum(spec, a, b, precision=HIGH, preferred_element_type=F32)


def body(gate_in, out_gate, value_in, out_grad, skip_gain, filter_taps):
    seq_n = lax.axis_size("seq")
    chan_n = lax.axis_size("chan")
    rows, local_ch = gate_in.shape
    filters = filter_taps.shape[1]
    dev_n = seq_n * chan_n
    per_dev = local_ch // dev_n
    part = rows // chan_n
    assert local_ch == filters and local_ch % dev_n == 0 and rows % chan_n == 0
    length = 2 * seq_n * rows
    k1 = seq_n + 1
    span = per_dev * rows
    cc = chan_n * per_dev
    pad_w = 128

    chan_id = lax.axis_index("chan")
    taps_rows = lax.dynamic_slice_in_dim(filter_taps, chan_id * part, part, axis=0)
    taps_send = taps_rows.T.reshape(per_dev, dev_n, part).transpose(1, 0, 2).reshape(dev_n, per_dev * part)

    lane = 128
    send_w = (2 * span + per_dev * part) // lane
    back_w = (3 * span + pad_w) // lane
    rq = rows // lane

    def prep_kernel(gi, vi, og, ot, tr, send):
        for f2 in range(per_dev):
            lanes = pl.ds(f2 * dev_n, dev_n)
            m = (gi[:, lanes].astype(F32) * vi[:, lanes].astype(F32)).astype(jnp.bfloat16).astype(F32).T
            g = (og[:, lanes].astype(F32) * ot[:, lanes].astype(F32)).astype(jnp.bfloat16).astype(F32).T
            for q in range(rq):
                send[pl.ds(f2 * rq + q, dev_n, stride=send_w), :] = m[:, q * lane : (q + 1) * lane]
                send[pl.ds((per_dev + f2) * rq + q, dev_n, stride=send_w), :] = g[:, q * lane : (q + 1) * lane]
        send[pl.ds(2 * per_dev * rq, dev_n, stride=send_w), :] = tr[...]

    send = pl.pallas_call(
        prep_kernel,
        out_shape=jax.ShapeDtypeStruct((dev_n * send_w, lane), F32),
        cost_estimate=pl.CostEstimate(flops=4 * rows * local_ch, transcendentals=0, bytes_accessed=4 * 2 * rows * local_ch * 2),
    )(gate_in, value_in, out_grad, out_gate, taps_send).reshape(dev_n, send_w * lane)
    recv = lax.all_to_all(send, ("seq", "chan"), 0, 0, tiled=True).reshape(seq_n, chan_n, -1)

    qn = rows // lane
    blocks = seq_n * qn
    k1 = blocks + 1
    length = 2 * blocks * lane
    recv = recv.reshape(seq_n, chan_n, send_w, lane)

    def by_block(field):
        part_rows = recv[:, :, field * per_dev * qn : (field + 1) * per_dev * qn]
        part_rows = part_rows.reshape(seq_n, chan_n, per_dev, qn, lane).transpose(0, 3, 2, 1, 4)
        return part_rows.reshape(blocks, cc, lane)

    m_pos = by_block(0)
    g_pos = by_block(1)
    h_pos = recv[:, :, 2 * per_dev * qn].reshape(seq_n, qn, lane // part, per_dev, part)
    h_pos = h_pos.transpose(0, 1, 3, 2, 4).reshape(blocks, per_dev, lane)
    skip_mine = jnp.sum(m_pos * g_pos, axis=(0, 2)).reshape(per_dev, chan_n).T

    c1, s1 = trig(k1, blocks, 2 * blocks)
    tw_c, tw_s = trig(k1, lane, length)
    tw_c = tw_c[:, None, :]
    tw_s = tw_s[:, None, :]
    c2, s2 = trig(lane, lane, lane)
    w_fwd = jnp.concatenate(
        [jnp.concatenate([c2, -s2], axis=1), jnp.concatenate([s2, c2], axis=1)], axis=0
    )
    w_inv = jnp.concatenate(
        [jnp.concatenate([c2, s2], axis=1), jnp.concatenate([-s2, c2], axis=1)], axis=0
    )
    weight = jnp.where(
        (lax.iota(jnp.int32, k1) == 0) | (lax.iota(jnp.int32, k1) == blocks), 1.0, 2.0
    ) / length
    ci, si = trig(blocks, k1, 2 * blocks)
    ci = ci * weight[None, :]
    si = si * weight[None, :]

    fields = jnp.concatenate([m_pos, g_pos, h_pos], axis=1)
    are = mm("ks,scr->kcr", c1, fields)
    aim = mm("ks,scr->kcr", -s1, fields)
    turned = jnp.concatenate([are * tw_c + aim * tw_s, aim * tw_c - are * tw_s], axis=2)
    spec = mm("kcn,nm->kcm", turned, w_fwd)

    mre, mim = spec[:, :cc, :lane], spec[:, :cc, lane:]
    gre, gim = spec[:, cc : 2 * cc, :lane], spec[:, cc : 2 * cc, lane:]
    h = spec[:, 2 * cc :]
    h = jnp.broadcast_to(h[:, :, None, :], (k1, per_dev, chan_n, 2 * lane)).reshape(k1, cc, 2 * lane)
    hre, him = h[:, :, :lane], h[:, :, lane:]

    conv_s = jnp.concatenate([hre * mre - him * mim, hre * mim + him * mre], axis=2)
    corr_s = jnp.concatenate([gre * hre + gim * him, gim * hre - gre * him], axis=2)
    taps_s = jnp.concatenate([gre * mre + gim * mim, gim * mre - gre * mim], axis=2)
    taps_s = jnp.sum(taps_s.reshape(k1, per_dev, chan_n, 2 * lane), axis=2)

    prod = jnp.concatenate([conv_s, corr_s, taps_s], axis=1)
    z = mm("kcn,nm->kcm", prod, w_inv)
    zre, zim = z[:, :, :lane], z[:, :, lane:]
    ure = zre * tw_c - zim * tw_s
    uim = zre * tw_s + zim * tw_c
    y = mm("ik,kcr->icr", ci, ure) - mm("ik,kcr->icr", si, uim)

    def by_chunk(block, copies):
        block = block.reshape(seq_n, qn, per_dev, copies, lane).transpose(0, 3, 2, 1, 4)
        return block.reshape(seq_n, copies, span)

    conv_blk = by_chunk(y[:, :cc], chan_n)
    corr_blk = by_chunk(y[:, cc : 2 * cc], chan_n)
    taps_blk = jnp.broadcast_to(by_chunk(y[:, 2 * cc :], 1), (seq_n, chan_n, span))
    skip_blk = jnp.broadcast_to(
        jnp.pad(skip_mine, ((0, 0), (0, pad_w - per_dev)))[None], (seq_n, chan_n, pad_w)
    )
    out_send = jnp.concatenate([conv_blk, corr_blk, taps_blk, skip_blk], axis=2)
    back = lax.all_to_all(out_send.reshape(dev_n, -1), ("seq", "chan"), 0, 0, tiled=True)

    def tail_kernel(bk, gi, vi, og, ot, sg, o_gg, o_gog, o_gv, o_taps, o_skip):
        def field(first):
            parts = [bk[pl.ds(first + q, dev_n, stride=back_w), :] for q in range(rq)]
            return jnp.concatenate(parts, axis=1).T

        for f2 in range(per_dev):
            lanes = pl.ds(f2 * dev_n, dev_n)
            conv = field(f2 * rq)
            corr = field((per_dev + f2) * rq)
            o_taps[:, lanes] = field((2 * per_dev + f2) * rq)
            gate = gi[:, lanes].astype(F32)
            val = vi[:, lanes].astype(F32)
            outg = og[:, lanes].astype(F32)
            m = (gate * val).astype(jnp.bfloat16).astype(F32)
            g = (outg * ot[:, lanes].astype(F32)).astype(jnp.bfloat16).astype(F32)
            s = sg[:, lanes]
            o_gog[:, lanes] = (outg * (conv + s * m)).astype(jnp.bfloat16)
            mix = corr + s * g
            o_gg[:, lanes] = (mix * val).astype(jnp.bfloat16)
            o_gv[:, lanes] = (mix * gate).astype(jnp.bfloat16)
        o_skip[...] = bk[pl.ds(3 * per_dev * rq, dev_n, stride=back_w), :].T[:per_dev, :]

    grad_shape = jax.ShapeDtypeStruct((rows, local_ch), jnp.bfloat16)
    grad_gate, grad_out_gate, grad_value, taps_grad, skip_two = pl.pallas_call(
        tail_kernel,
        out_shape=(
            grad_shape,
            grad_shape,
            grad_shape,
            jax.ShapeDtypeStruct((rows, filters), F32),
            jax.ShapeDtypeStruct((per_dev, dev_n), F32),
        ),
        cost_estimate=pl.CostEstimate(flops=12 * rows * local_ch, transcendentals=0, bytes_accessed=4 * 4 * rows * local_ch * 2),
    )(back.reshape(dev_n * back_w, lane), gate_in, value_in, out_grad, out_gate, skip_gain.reshape(1, local_ch))
    skip_grad = skip_two.reshape(local_ch)
    return (grad_gate, grad_out_gate, grad_value, skip_grad, taps_grad)


def solution(mesh):
    placed = (
        P("seq", "chan"),
        P("seq", "chan"),
        P("seq", "chan"),
        P("seq", "chan"),
        P("chan"),
        P("seq", None),
    )
    return jax.shard_map(
        body,
        mesh=mesh,
        in_specs=placed,
        out_specs=(P("seq", "chan"), P("seq", "chan"), P("seq", "chan"), P("chan"), P("seq", None)),
        check_vma=False,
    )
```

```python
import math

import jax
import jax.numpy as jnp
from jax import lax
from jax.experimental import pallas as pl
from jax.experimental.pallas import tpu as pltpu
from jax.sharding import PartitionSpec as P

HIGH = lax.Precision.HIGH
F32 = jnp.float32


def trig(a_count, b_count, period, scale=1.0):
    a_ids = lax.iota(jnp.int32, a_count)[:, None]
    b_ids = lax.iota(jnp.int32, b_count)[None, :]
    turns = (a_ids * b_ids) % period
    angle = turns.astype(F32) * (2.0 * math.pi / period)
    return jnp.cos(angle) * scale, jnp.sin(angle) * scale


def mm(spec, a, b):
    return jnp.einsum(spec, a, b, precision=HIGH, preferred_element_type=F32)


def body(gate_in, out_gate, value_in, out_grad, skip_gain, filter_taps):
    seq_n = lax.axis_size("seq")
    chan_n = lax.axis_size("chan")
    rows, local_ch = gate_in.shape
    filters = filter_taps.shape[1]
    dev_n = seq_n * chan_n
    per_dev = local_ch // dev_n
    part = rows // chan_n
    assert local_ch == filters and local_ch % dev_n == 0 and rows % chan_n == 0
    length = 2 * seq_n * rows
    k1 = seq_n + 1
    span = per_dev * rows
    cc = chan_n * per_dev
    pad_w = 128


    lane = 128
    send_w = (2 * span + per_dev * part) // lane
    back_w = (3 * span + pad_w) // lane
    rq = rows // lane

    def prep_kernel(gi, vi, og, ot, ft, send):
        for f2 in range(per_dev):
            lanes = pl.ds(f2 * dev_n, dev_n)
            m = (gi[:, lanes].astype(F32) * vi[:, lanes].astype(F32)).astype(jnp.bfloat16).astype(F32).T
            g = (og[:, lanes].astype(F32) * ot[:, lanes].astype(F32)).astype(jnp.bfloat16).astype(F32).T
            for q in range(rq):
                send[pl.ds(f2 * rq + q, dev_n, stride=send_w), :] = m[:, q * lane : (q + 1) * lane]
                send[pl.ds((per_dev + f2) * rq + q, dev_n, stride=send_w), :] = g[:, q * lane : (q + 1) * lane]
        first = pl.multiple_of(lax.axis_index("chan") * part, part)
        window = jnp.concatenate(
            [ft[pl.ds(first, part), pl.ds(f2 * dev_n, dev_n)] for f2 in range(per_dev)], axis=0
        )
        send[pl.ds(2 * per_dev * rq, dev_n, stride=send_w), :] = window.T

    send = pl.pallas_call(
        prep_kernel,
        out_shape=jax.ShapeDtypeStruct((dev_n * send_w, lane), F32),
        cost_estimate=pl.CostEstimate(flops=4 * rows * local_ch, transcendentals=0, bytes_accessed=4 * 2 * rows * local_ch * 2),
    )(gate_in, value_in, out_grad, out_gate, filter_taps).reshape(dev_n, send_w * lane)
    recv = lax.all_to_all(send, ("seq", "chan"), 0, 0, tiled=True).reshape(seq_n, chan_n, -1)

    qn = rows // lane
    blocks = seq_n * qn
    k1 = blocks + 1
    length = 2 * blocks * lane
    recv = recv.reshape(seq_n, chan_n, send_w, lane)

    def by_block(field):
        part_rows = recv[:, :, field * per_dev * qn : (field + 1) * per_dev * qn]
        part_rows = part_rows.reshape(seq_n, chan_n, per_dev, qn, lane).transpose(0, 3, 2, 1, 4)
        return part_rows.reshape(blocks, cc, lane)

    m_pos = by_block(0)
    g_pos = by_block(1)
    h_pos = recv[:, :, 2 * per_dev * qn].reshape(seq_n, qn, lane // part, per_dev, part)
    h_pos = h_pos.transpose(0, 1, 3, 2, 4).reshape(blocks, per_dev, lane)
    skip_mine = jnp.sum(m_pos * g_pos, axis=(0, 2)).reshape(per_dev, chan_n).T

    c1, s1 = trig(k1, blocks, 2 * blocks)
    tw_c, tw_s = trig(k1, lane, length)
    tw_c = tw_c[:, None, :]
    tw_s = tw_s[:, None, :]
    c2, s2 = trig(lane, lane, lane)
    w_fwd = jnp.concatenate(
        [jnp.concatenate([c2, -s2], axis=1), jnp.concatenate([s2, c2], axis=1)], axis=0
    )
    w_inv = jnp.concatenate(
        [jnp.concatenate([c2, s2], axis=1), jnp.concatenate([-s2, c2], axis=1)], axis=0
    )
    weight = jnp.where(
        (lax.iota(jnp.int32, k1) == 0) | (lax.iota(jnp.int32, k1) == blocks), 1.0, 2.0
    ) / length
    ci, si = trig(blocks, k1, 2 * blocks)
    ci = ci * weight[None, :]
    si = si * weight[None, :]

    fields = jnp.concatenate([m_pos, g_pos, h_pos], axis=1)
    are = mm("ks,scr->kcr", c1, fields)
    aim = mm("ks,scr->kcr", -s1, fields)
    turned = jnp.concatenate([are * tw_c + aim * tw_s, aim * tw_c - are * tw_s], axis=2)
    spec = mm("kcn,nm->kcm", turned, w_fwd)

    mre, mim = spec[:, :cc, :lane], spec[:, :cc, lane:]
    gre, gim = spec[:, cc : 2 * cc, :lane], spec[:, cc : 2 * cc, lane:]
    h = spec[:, 2 * cc :]
    h = jnp.broadcast_to(h[:, :, None, :], (k1, per_dev, chan_n, 2 * lane)).reshape(k1, cc, 2 * lane)
    hre, him = h[:, :, :lane], h[:, :, lane:]

    conv_s = jnp.concatenate([hre * mre - him * mim, hre * mim + him * mre], axis=2)
    corr_s = jnp.concatenate([gre * hre + gim * him, gim * hre - gre * him], axis=2)
    taps_s = jnp.concatenate([gre * mre + gim * mim, gim * mre - gre * mim], axis=2)
    taps_s = jnp.sum(taps_s.reshape(k1, per_dev, chan_n, 2 * lane), axis=2)

    prod = jnp.concatenate([conv_s, corr_s, taps_s], axis=1)
    z = mm("kcn,nm->kcm", prod, w_inv)
    zre, zim = z[:, :, :lane], z[:, :, lane:]
    ure = zre * tw_c - zim * tw_s
    uim = zre * tw_s + zim * tw_c
    y = mm("ik,kcr->icr", ci, ure) - mm("ik,kcr->icr", si, uim)

    def by_chunk(block, copies):
        block = block.reshape(seq_n, qn, per_dev, copies, lane).transpose(0, 3, 2, 1, 4)
        return block.reshape(seq_n, copies, span)

    conv_blk = by_chunk(y[:, :cc], chan_n)
    corr_blk = by_chunk(y[:, cc : 2 * cc], chan_n)
    taps_blk = jnp.broadcast_to(by_chunk(y[:, 2 * cc :], 1), (seq_n, chan_n, span))
    skip_blk = jnp.broadcast_to(
        jnp.pad(skip_mine, ((0, 0), (0, pad_w - per_dev)))[None], (seq_n, chan_n, pad_w)
    )
    out_send = jnp.concatenate([conv_blk, corr_blk, taps_blk, skip_blk], axis=2)
    back = lax.all_to_all(out_send.reshape(dev_n, -1), ("seq", "chan"), 0, 0, tiled=True)

    def tail_kernel(bk, gi, vi, og, ot, sg, o_gg, o_gog, o_gv, o_taps, o_skip):
        def field(first):
            parts = [bk[pl.ds(first + q, dev_n, stride=back_w), :] for q in range(rq)]
            return jnp.concatenate(parts, axis=1).T

        for f2 in range(per_dev):
            lanes = pl.ds(f2 * dev_n, dev_n)
            conv = field(f2 * rq)
            corr = field((per_dev + f2) * rq)
            o_taps[:, lanes] = field((2 * per_dev + f2) * rq)
            gate = gi[:, lanes].astype(F32)
            val = vi[:, lanes].astype(F32)
            outg = og[:, lanes].astype(F32)
            m = (gate * val).astype(jnp.bfloat16).astype(F32)
            g = (outg * ot[:, lanes].astype(F32)).astype(jnp.bfloat16).astype(F32)
            s = sg[:, lanes]
            o_gog[:, lanes] = (outg * (conv + s * m)).astype(jnp.bfloat16)
            mix = corr + s * g
            o_gg[:, lanes] = (mix * val).astype(jnp.bfloat16)
            o_gv[:, lanes] = (mix * gate).astype(jnp.bfloat16)
        o_skip[...] = bk[pl.ds(3 * per_dev * rq, dev_n, stride=back_w), :].T[:per_dev, :]

    grad_shape = jax.ShapeDtypeStruct((rows, local_ch), jnp.bfloat16)
    grad_gate, grad_out_gate, grad_value, taps_grad, skip_two = pl.pallas_call(
        tail_kernel,
        out_shape=(
            grad_shape,
            grad_shape,
            grad_shape,
            jax.ShapeDtypeStruct((rows, filters), F32),
            jax.ShapeDtypeStruct((per_dev, dev_n), F32),
        ),
        cost_estimate=pl.CostEstimate(flops=12 * rows * local_ch, transcendentals=0, bytes_accessed=4 * 4 * rows * local_ch * 2),
    )(back.reshape(dev_n * back_w, lane), gate_in, value_in, out_grad, out_gate, skip_gain.reshape(1, local_ch))
    skip_grad = skip_two.reshape(local_ch)
    return (grad_gate, grad_out_gate, grad_value, skip_grad, taps_grad)


def solution(mesh):
    placed = (
        P("seq", "chan"),
        P("seq", "chan"),
        P("seq", "chan"),
        P("seq", "chan"),
        P("chan"),
        P("seq", None),
    )
    return jax.shard_map(
        body,
        mesh=mesh,
        in_specs=placed,
        out_specs=(P("seq", "chan"), P("seq", "chan"), P("seq", "chan"), P("chan"), P("seq", None)),
        check_vma=False,
    )
```

```python
import math

import jax
import jax.numpy as jnp
from jax import lax
from jax.experimental import pallas as pl
from jax.experimental.pallas import tpu as pltpu
from jax.sharding import PartitionSpec as P

HIGH = lax.Precision.HIGH
F32 = jnp.float32


def trig(a_count, b_count, period, scale=1.0):
    a_ids = lax.iota(jnp.int32, a_count)[:, None]
    b_ids = lax.iota(jnp.int32, b_count)[None, :]
    turns = (a_ids * b_ids) % period
    angle = turns.astype(F32) * (2.0 * math.pi / period)
    return jnp.cos(angle) * scale, jnp.sin(angle) * scale


def mm(spec, a, b):
    return jnp.einsum(spec, a, b, precision=HIGH, preferred_element_type=F32)


def body(gate_in, out_gate, value_in, out_grad, skip_gain, filter_taps):
    seq_n = lax.axis_size("seq")
    chan_n = lax.axis_size("chan")
    rows, local_ch = gate_in.shape
    filters = filter_taps.shape[1]
    dev_n = seq_n * chan_n
    per_dev = local_ch // dev_n
    part = rows // chan_n
    assert local_ch == filters and local_ch % dev_n == 0 and rows % chan_n == 0
    length = 2 * seq_n * rows
    k1 = seq_n + 1
    span = per_dev * rows
    cc = chan_n * per_dev
    pad_w = 128


    lane = 128
    send_w = (2 * span + per_dev * part) // lane
    back_w = (3 * span + pad_w) // lane
    rq = rows // lane

    def prep_kernel(gi, vi, og, ot, ft, send):
        for f2 in range(per_dev):
            lanes = pl.ds(f2 * dev_n, dev_n)
            m = (gi[:, lanes].astype(F32) * vi[:, lanes].astype(F32)).astype(jnp.bfloat16).astype(F32).T
            g = (og[:, lanes].astype(F32) * ot[:, lanes].astype(F32)).astype(jnp.bfloat16).astype(F32).T
            for q in range(rq):
                send[pl.ds(f2 * rq + q, dev_n, stride=send_w), :] = m[:, q * lane : (q + 1) * lane]
                send[pl.ds((per_dev + f2) * rq + q, dev_n, stride=send_w), :] = g[:, q * lane : (q + 1) * lane]
        first = pl.multiple_of(lax.axis_index("chan") * part, part)
        window = jnp.concatenate(
            [ft[pl.ds(first, part), pl.ds(f2 * dev_n, dev_n)] for f2 in range(per_dev)], axis=0
        )
        send[pl.ds(2 * per_dev * rq, dev_n, stride=send_w), :] = window.T

    send = pl.pallas_call(
        prep_kernel,
        out_shape=jax.ShapeDtypeStruct((dev_n * send_w, lane), F32),
        cost_estimate=pl.CostEstimate(flops=4 * rows * local_ch, transcendentals=0, bytes_accessed=4 * 2 * rows * local_ch * 2),
    )(gate_in, value_in, out_grad, out_gate, filter_taps).reshape(dev_n, send_w * lane)
    recv = lax.all_to_all(send, ("seq", "chan"), 0, 0, tiled=True).reshape(seq_n, chan_n, -1)

    qn = rows // lane
    blocks = seq_n * qn
    k1 = blocks + 1
    length = 2 * blocks * lane
    recv = recv.reshape(seq_n, chan_n, send_w, lane)

    def by_block(field):
        part_rows = recv[:, :, field * per_dev * qn : (field + 1) * per_dev * qn]
        part_rows = part_rows.reshape(seq_n, chan_n, per_dev, qn, lane).transpose(0, 3, 2, 1, 4)
        return part_rows.reshape(blocks, cc, lane)

    m_pos = by_block(0)
    g_pos = by_block(1)
    h_pos = recv[:, :, 2 * per_dev * qn].reshape(seq_n, qn, lane // part, per_dev, part)
    h_pos = h_pos.transpose(0, 1, 3, 2, 4).reshape(blocks, per_dev, lane)
    skip_mine = jnp.sum(m_pos * g_pos, axis=(0, 2)).reshape(per_dev, chan_n).T

    c1, s1 = trig(k1, blocks, 2 * blocks)
    tw_c, tw_s = trig(k1, lane, length)
    tw_c = tw_c[:, None, :]
    tw_s = tw_s[:, None, :]
    c2, s2 = trig(lane, lane, lane)
    w_fwd = jnp.concatenate(
        [jnp.concatenate([c2, -s2], axis=1), jnp.concatenate([s2, c2], axis=1)], axis=0
    )
    w_inv = jnp.concatenate(
        [jnp.concatenate([c2, s2], axis=1), jnp.concatenate([-s2, c2], axis=1)], axis=0
    )
    weight = jnp.where(
        (lax.iota(jnp.int32, k1) == 0) | (lax.iota(jnp.int32, k1) == blocks), 1.0, 2.0
    ) / length
    ci, si = trig(blocks, k1, 2 * blocks)
    ci = ci * weight[None, :]
    si = si * weight[None, :]

    fields = jnp.concatenate([m_pos, g_pos, h_pos], axis=1)
    are = mm("ks,scr->kcr", c1, fields)
    aim = mm("ks,scr->kcr", -s1, fields)
    turned = jnp.concatenate([are * tw_c + aim * tw_s, aim * tw_c - are * tw_s], axis=2)
    spec = mm("kcn,nm->kcm", turned, w_fwd)

    mre, mim = spec[:, :cc, :lane], spec[:, :cc, lane:]
    gre, gim = spec[:, cc : 2 * cc, :lane], spec[:, cc : 2 * cc, lane:]
    h = spec[:, 2 * cc :]
    h = jnp.broadcast_to(h[:, :, None, :], (k1, per_dev, chan_n, 2 * lane)).reshape(k1, cc, 2 * lane)
    hre, him = h[:, :, :lane], h[:, :, lane:]

    conv_s = jnp.concatenate([hre * mre - him * mim, hre * mim + him * mre], axis=2)
    corr_s = jnp.concatenate([gre * hre + gim * him, gim * hre - gre * him], axis=2)
    taps_s = jnp.concatenate([gre * mre + gim * mim, gim * mre - gre * mim], axis=2)
    taps_s = jnp.sum(taps_s.reshape(k1, per_dev, chan_n, 2 * lane), axis=2)

    prod = jnp.concatenate([conv_s, corr_s, taps_s], axis=1)
    z = mm("kcn,nm->kcm", prod, w_inv)
    zre, zim = z[:, :, :lane], z[:, :, lane:]
    ure = zre * tw_c - zim * tw_s
    uim = zre * tw_s + zim * tw_c
    y = mm("ik,kcr->icr", ci, ure) - mm("ik,kcr->icr", si, uim)

    def by_chunk(block, copies):
        block = block.reshape(seq_n, qn, per_dev, copies, lane).transpose(0, 3, 2, 1, 4)
        return block.reshape(seq_n, copies, span)

    conv_blk = by_chunk(y[:, :cc], chan_n)
    corr_blk = by_chunk(y[:, cc : 2 * cc], chan_n)
    taps_blk = jnp.broadcast_to(by_chunk(y[:, 2 * cc :], 1), (seq_n, chan_n, span))
    skip_blk = jnp.broadcast_to(
        jnp.pad(skip_mine, ((0, 0), (0, pad_w - per_dev)))[None], (seq_n, chan_n, pad_w)
    )
    out_send = jnp.concatenate([conv_blk, corr_blk, taps_blk, skip_blk], axis=2)
    back = lax.all_to_all(out_send.reshape(dev_n, -1), ("seq", "chan"), 0, 0, tiled=True)

    def tail_kernel(bk, gi, vi, og, ot, sg, o_gg, o_gog, o_gv, o_taps, o_skip):
        f2 = pl.program_id(0)

        def field(first):
            parts = [bk[pl.ds(first + q, dev_n, stride=back_w), :] for q in range(rq)]
            return jnp.concatenate(parts, axis=1).T

        conv = field(f2 * rq)
        corr = field((per_dev + f2) * rq)
        o_taps[...] = field((2 * per_dev + f2) * rq)
        gate = gi[...].astype(F32)
        val = vi[...].astype(F32)
        outg = og[...].astype(F32)
        m = (gate * val).astype(jnp.bfloat16).astype(F32)
        g = (outg * ot[...].astype(F32)).astype(jnp.bfloat16).astype(F32)
        s = sg[...]
        o_gog[...] = (outg * (conv + s * m)).astype(jnp.bfloat16)
        mix = corr + s * g
        o_gg[...] = (mix * val).astype(jnp.bfloat16)
        o_gv[...] = (mix * gate).astype(jnp.bfloat16)

        @pl.when(f2 == 0)
        def _():
            o_skip[...] = bk[pl.ds(3 * per_dev * rq, dev_n, stride=back_w), :].T[:8, :]

    half = pl.BlockSpec((rows, dev_n), lambda f: (0, f))
    grad_shape = jax.ShapeDtypeStruct((rows, local_ch), jnp.bfloat16)
    grad_gate, grad_out_gate, grad_value, taps_grad, skip_rows = pl.pallas_call(
        tail_kernel,
        grid=(per_dev,),
        in_specs=[
            pl.BlockSpec((dev_n * back_w, lane), lambda f: (0, 0)),
            half,
            half,
            half,
            half,
            pl.BlockSpec((1, dev_n), lambda f: (0, f)),
        ],
        out_specs=(half, half, half, half, pl.BlockSpec((8, dev_n), lambda f: (0, 0))),
        out_shape=(
            grad_shape,
            grad_shape,
            grad_shape,
            jax.ShapeDtypeStruct((rows, filters), F32),
            jax.ShapeDtypeStruct((8, dev_n), F32),
        ),
        cost_estimate=pl.CostEstimate(flops=12 * rows * local_ch, transcendentals=0, bytes_accessed=4 * 4 * rows * local_ch * 2),
    )(back.reshape(dev_n * back_w, lane), gate_in, value_in, out_grad, out_gate, skip_gain.reshape(1, local_ch))
    skip_two = skip_rows[:per_dev]
    skip_grad = skip_two.reshape(local_ch)
    return (grad_gate, grad_out_gate, grad_value, skip_grad, taps_grad)


def solution(mesh):
    placed = (
        P("seq", "chan"),
        P("seq", "chan"),
        P("seq", "chan"),
        P("seq", "chan"),
        P("chan"),
        P("seq", None),
    )
    return jax.shard_map(
        body,
        mesh=mesh,
        in_specs=placed,
        out_specs=(P("seq", "chan"), P("seq", "chan"), P("seq", "chan"), P("chan"), P("seq", None)),
        check_vma=False,
    )
```

```python
import math

import jax
import jax.numpy as jnp
from jax import lax
from jax.experimental import pallas as pl
from jax.experimental.pallas import tpu as pltpu
from jax.sharding import PartitionSpec as P

HIGH = lax.Precision.HIGH
F32 = jnp.float32


def trig(a_count, b_count, period, scale=1.0):
    a_ids = lax.iota(jnp.int32, a_count)[:, None]
    b_ids = lax.iota(jnp.int32, b_count)[None, :]
    turns = (a_ids * b_ids) % period
    angle = turns.astype(F32) * (2.0 * math.pi / period)
    return jnp.cos(angle) * scale, jnp.sin(angle) * scale


def mm(spec, a, b):
    return jnp.einsum(spec, a, b, precision=HIGH, preferred_element_type=F32)


def body(gate_in, out_gate, value_in, out_grad, skip_gain, filter_taps):
    seq_n = lax.axis_size("seq")
    chan_n = lax.axis_size("chan")
    rows, local_ch = gate_in.shape
    filters = filter_taps.shape[1]
    dev_n = seq_n * chan_n
    per_dev = local_ch // dev_n
    part = rows // chan_n
    assert local_ch == filters and local_ch % dev_n == 0 and rows % chan_n == 0
    length = 2 * seq_n * rows
    k1 = seq_n + 1
    span = per_dev * rows
    cc = chan_n * per_dev
    pad_w = 128


    lane = 128
    send_w = (2 * span + per_dev * part) // lane
    back_w = (3 * span + pad_w) // lane
    rq = rows // lane

    def prep_kernel(gi, vi, og, ot, ft, send):
        for f2 in range(per_dev):
            lanes = pl.ds(f2 * dev_n, dev_n)
            m = (gi[:, lanes].astype(F32) * vi[:, lanes].astype(F32)).astype(jnp.bfloat16).astype(F32).T
            g = (og[:, lanes].astype(F32) * ot[:, lanes].astype(F32)).astype(jnp.bfloat16).astype(F32).T
            for q in range(rq):
                send[pl.ds(f2 * rq + q, dev_n, stride=send_w), :] = m[:, q * lane : (q + 1) * lane]
                send[pl.ds((per_dev + f2) * rq + q, dev_n, stride=send_w), :] = g[:, q * lane : (q + 1) * lane]
        first = pl.multiple_of(lax.axis_index("chan") * part, part)
        window = jnp.concatenate(
            [ft[pl.ds(first, part), pl.ds(f2 * dev_n, dev_n)] for f2 in range(per_dev)], axis=0
        )
        send[pl.ds(2 * per_dev * rq, dev_n, stride=send_w), :] = window.T

    send = pl.pallas_call(
        prep_kernel,
        out_shape=jax.ShapeDtypeStruct((dev_n * send_w, lane), F32),
        cost_estimate=pl.CostEstimate(flops=4 * rows * local_ch, transcendentals=0, bytes_accessed=4 * 2 * rows * local_ch * 2),
    )(gate_in, value_in, out_grad, out_gate, filter_taps).reshape(dev_n, send_w * lane)
    recv = lax.all_to_all(send, ("seq", "chan"), 0, 0, tiled=True).reshape(seq_n, chan_n, -1)

    qn = rows // lane
    blocks = seq_n * qn
    k1 = blocks + 1
    length = 2 * blocks * lane
    recv = recv.reshape(seq_n, chan_n, send_w, lane)

    def by_block(field):
        part_rows = recv[:, :, field * per_dev * qn : (field + 1) * per_dev * qn]
        part_rows = part_rows.reshape(seq_n, chan_n, per_dev, qn, lane).transpose(0, 3, 2, 1, 4)
        return part_rows.reshape(blocks, cc, lane)

    m_pos = by_block(0)
    g_pos = by_block(1)
    h_pos = recv[:, :, 2 * per_dev * qn].reshape(seq_n, qn, lane // part, per_dev, part)
    h_pos = h_pos.transpose(0, 1, 3, 2, 4).reshape(blocks, per_dev, lane)
    skip_mine = jnp.sum(m_pos * g_pos, axis=(0, 2)).reshape(per_dev, chan_n).T

    k1_true = k1
    k1 = -(-k1_true // 8) * 8
    live = (lax.iota(jnp.int32, k1) < k1_true).astype(F32)[:, None]
    c1, s1 = trig(k1, blocks, 2 * blocks)
    w1 = jnp.concatenate([c1 * live, -s1 * live], axis=0)
    tw_c, tw_s = trig(k1, lane, length)
    tw_c = tw_c[:, None, :]
    tw_s = tw_s[:, None, :]
    c2, s2 = trig(lane, lane, lane)
    w_fwd = jnp.concatenate(
        [jnp.concatenate([c2, -s2], axis=1), jnp.concatenate([s2, c2], axis=1)], axis=0
    )
    w_inv = jnp.concatenate(
        [jnp.concatenate([c2, s2], axis=1), jnp.concatenate([-s2, c2], axis=1)], axis=0
    )
    rows_k = lax.iota(jnp.int32, k1)
    weight = jnp.where((rows_k == 0) | (rows_k == blocks), 1.0, 2.0)
    weight = jnp.where(rows_k < k1_true, weight, 0.0) / length
    ci, si = trig(blocks, k1, 2 * blocks)
    wi = jnp.concatenate([ci * weight[None, :], -si * weight[None, :]], axis=1)

    fields = jnp.concatenate([m_pos, g_pos, h_pos], axis=1)
    a = mm("ks,scr->kcr", w1, fields)
    are, aim = a[:k1], a[k1:]
    turned = jnp.concatenate([are * tw_c + aim * tw_s, aim * tw_c - are * tw_s], axis=2)
    spec = mm("kcn,nm->kcm", turned, w_fwd)

    mre, mim = spec[:, :cc, :lane], spec[:, :cc, lane:]
    gre, gim = spec[:, cc : 2 * cc, :lane], spec[:, cc : 2 * cc, lane:]
    h = spec[:, 2 * cc :]
    h = jnp.broadcast_to(h[:, :, None, :], (k1, per_dev, chan_n, 2 * lane)).reshape(k1, cc, 2 * lane)
    hre, him = h[:, :, :lane], h[:, :, lane:]

    conv_s = jnp.concatenate([hre * mre - him * mim, hre * mim + him * mre], axis=2)
    corr_s = jnp.concatenate([gre * hre + gim * him, gim * hre - gre * him], axis=2)
    taps_s = jnp.concatenate([gre * mre + gim * mim, gim * mre - gre * mim], axis=2)
    taps_s = jnp.sum(taps_s.reshape(k1, per_dev, chan_n, 2 * lane), axis=2)

    prod = jnp.concatenate([conv_s, corr_s, taps_s], axis=1)
    z = mm("kcn,nm->kcm", prod, w_inv)
    zre, zim = z[:, :, :lane], z[:, :, lane:]
    ure = zre * tw_c - zim * tw_s
    uim = zre * tw_s + zim * tw_c
    y = mm("ik,kcr->icr", wi, jnp.concatenate([ure, uim], axis=0))

    def by_chunk(block, copies):
        block = block.reshape(seq_n, qn, per_dev, copies, lane).transpose(0, 3, 2, 1, 4)
        return block.reshape(seq_n, copies, span)

    conv_blk = by_chunk(y[:, :cc], chan_n)
    corr_blk = by_chunk(y[:, cc : 2 * cc], chan_n)
    taps_blk = jnp.broadcast_to(by_chunk(y[:, 2 * cc :], 1), (seq_n, chan_n, span))
    skip_blk = jnp.broadcast_to(
        jnp.pad(skip_mine, ((0, 0), (0, pad_w - per_dev)))[None], (seq_n, chan_n, pad_w)
    )
    out_send = jnp.concatenate([conv_blk, corr_blk, taps_blk, skip_blk], axis=2)
    back = lax.all_to_all(out_send.reshape(dev_n, -1), ("seq", "chan"), 0, 0, tiled=True)

    def tail_kernel(bk, gi, vi, og, ot, sg, o_gg, o_gog, o_gv, o_taps, o_skip):
        def field(first):
            parts = [bk[pl.ds(first + q, dev_n, stride=back_w), :] for q in range(rq)]
            return jnp.concatenate(parts, axis=1).T

        for f2 in range(per_dev):
            lanes = pl.ds(f2 * dev_n, dev_n)
            conv = field(f2 * rq)
            corr = field((per_dev + f2) * rq)
            o_taps[:, lanes] = field((2 * per_dev + f2) * rq)
            gate = gi[:, lanes].astype(F32)
            val = vi[:, lanes].astype(F32)
            outg = og[:, lanes].astype(F32)
            m = (gate * val).astype(jnp.bfloat16).astype(F32)
            g = (outg * ot[:, lanes].astype(F32)).astype(jnp.bfloat16).astype(F32)
            s = sg[:, lanes]
            o_gog[:, lanes] = (outg * (conv + s * m)).astype(jnp.bfloat16)
            mix = corr + s * g
            o_gg[:, lanes] = (mix * val).astype(jnp.bfloat16)
            o_gv[:, lanes] = (mix * gate).astype(jnp.bfloat16)
        o_skip[...] = bk[pl.ds(3 * per_dev * rq, dev_n, stride=back_w), :].T[:per_dev, :]

    grad_shape = jax.ShapeDtypeStruct((rows, local_ch), jnp.bfloat16)
    grad_gate, grad_out_gate, grad_value, taps_grad, skip_two = pl.pallas_call(
        tail_kernel,
        out_shape=(
            grad_shape,
            grad_shape,
            grad_shape,
            jax.ShapeDtypeStruct((rows, filters), F32),
            jax.ShapeDtypeStruct((per_dev, dev_n), F32),
        ),
        cost_estimate=pl.CostEstimate(flops=12 * rows * local_ch, transcendentals=0, bytes_accessed=4 * 4 * rows * local_ch * 2),
    )(back.reshape(dev_n * back_w, lane), gate_in, value_in, out_grad, out_gate, skip_gain.reshape(1, local_ch))
    skip_grad = skip_two.reshape(local_ch)
    return (grad_gate, grad_out_gate, grad_value, skip_grad, taps_grad)


def solution(mesh):
    placed = (
        P("seq", "chan"),
        P("seq", "chan"),
        P("seq", "chan"),
        P("seq", "chan"),
        P("chan"),
        P("seq", None),
    )
    return jax.shard_map(
        body,
        mesh=mesh,
        in_specs=placed,
        out_specs=(P("seq", "chan"), P("seq", "chan"), P("seq", "chan"), P("chan"), P("seq", None)),
        check_vma=False,
    )
```

```python
import math

import jax
import jax.numpy as jnp
from jax import lax
from jax.experimental import pallas as pl
from jax.experimental.pallas import tpu as pltpu
from jax.sharding import PartitionSpec as P

HIGH = lax.Precision.HIGH
F32 = jnp.float32


def trig(a_count, b_count, period, scale=1.0):
    a_ids = lax.iota(jnp.int32, a_count)[:, None]
    b_ids = lax.iota(jnp.int32, b_count)[None, :]
    turns = (a_ids * b_ids) % period
    angle = turns.astype(F32) * (2.0 * math.pi / period)
    return jnp.cos(angle) * scale, jnp.sin(angle) * scale


def mm(spec, a, b):
    return jnp.einsum(spec, a, b, precision=HIGH, preferred_element_type=F32)


def body(gate_in, out_gate, value_in, out_grad, skip_gain, filter_taps):
    seq_n = lax.axis_size("seq")
    chan_n = lax.axis_size("chan")
    rows, local_ch = gate_in.shape
    filters = filter_taps.shape[1]
    dev_n = seq_n * chan_n
    per_dev = local_ch // dev_n
    part = rows // chan_n
    assert local_ch == filters and local_ch % dev_n == 0 and rows % chan_n == 0
    length = 2 * seq_n * rows
    k1 = seq_n + 1
    span = per_dev * rows
    cc = chan_n * per_dev
    pad_w = 128


    lane = 128
    send_w = (2 * span + per_dev * part) // lane
    back_w = (3 * span + pad_w) // lane
    rq = rows // lane

    def prep_kernel(gi, vi, og, ot, ft, send, taps_buf, taps_sem):
        first = pl.multiple_of(lax.axis_index("chan") * part, part)
        taps_copy = pltpu.make_async_copy(ft.at[pl.ds(first, part), :], taps_buf, taps_sem)
        taps_copy.start()
        for f2 in range(per_dev):
            lanes = pl.ds(f2 * dev_n, dev_n)
            m = (gi[:, lanes].astype(F32) * vi[:, lanes].astype(F32)).astype(jnp.bfloat16).astype(F32).T
            g = (og[:, lanes].astype(F32) * ot[:, lanes].astype(F32)).astype(jnp.bfloat16).astype(F32).T
            for q in range(rq):
                send[pl.ds(f2 * rq + q, dev_n, stride=send_w), :] = m[:, q * lane : (q + 1) * lane]
                send[pl.ds((per_dev + f2) * rq + q, dev_n, stride=send_w), :] = g[:, q * lane : (q + 1) * lane]
        taps_copy.wait()
        window = jnp.concatenate(
            [taps_buf[:, pl.ds(f2 * dev_n, dev_n)] for f2 in range(per_dev)], axis=0
        )
        send[pl.ds(2 * per_dev * rq, dev_n, stride=send_w), :] = window.T

    send = pl.pallas_call(
        prep_kernel,
        out_shape=jax.ShapeDtypeStruct((dev_n * send_w, lane), F32),
        in_specs=[pl.BlockSpec(memory_space=pltpu.VMEM)] * 4 + [pl.BlockSpec(memory_space=pl.ANY)],
        out_specs=pl.BlockSpec(memory_space=pltpu.VMEM),
        scratch_shapes=[pltpu.VMEM((part, filters), F32), pltpu.SemaphoreType.DMA(())],
        cost_estimate=pl.CostEstimate(flops=4 * rows * local_ch, transcendentals=0, bytes_accessed=4 * 2 * rows * local_ch * 2),
    )(gate_in, value_in, out_grad, out_gate, filter_taps).reshape(dev_n, send_w * lane)
    recv = lax.all_to_all(send, ("seq", "chan"), 0, 0, tiled=True).reshape(seq_n, chan_n, -1)

    qn = rows // lane
    blocks = seq_n * qn
    k1 = blocks + 1
    length = 2 * blocks * lane
    recv = recv.reshape(seq_n, chan_n, send_w, lane)

    def by_block(field):
        part_rows = recv[:, :, field * per_dev * qn : (field + 1) * per_dev * qn]
        part_rows = part_rows.reshape(seq_n, chan_n, per_dev, qn, lane).transpose(0, 3, 2, 1, 4)
        return part_rows.reshape(blocks, cc, lane)

    m_pos = by_block(0)
    g_pos = by_block(1)
    h_pos = recv[:, :, 2 * per_dev * qn].reshape(seq_n, qn, lane // part, per_dev, part)
    h_pos = h_pos.transpose(0, 1, 3, 2, 4).reshape(blocks, per_dev, lane)
    skip_mine = jnp.sum(m_pos * g_pos, axis=(0, 2)).reshape(per_dev, chan_n).T

    k1_true = k1
    k1 = -(-k1_true // 8) * 8
    live = (lax.iota(jnp.int32, k1) < k1_true).astype(F32)[:, None]
    c1, s1 = trig(k1, blocks, 2 * blocks)
    w1 = jnp.concatenate([c1 * live, -s1 * live], axis=0)
    tw_c, tw_s = trig(k1, lane, length)
    tw_c = tw_c[:, None, :]
    tw_s = tw_s[:, None, :]
    c2, s2 = trig(lane, lane, lane)
    w_fwd = jnp.concatenate(
        [jnp.concatenate([c2, -s2], axis=1), jnp.concatenate([s2, c2], axis=1)], axis=0
    )
    w_inv = jnp.concatenate(
        [jnp.concatenate([c2, s2], axis=1), jnp.concatenate([-s2, c2], axis=1)], axis=0
    )
    rows_k = lax.iota(jnp.int32, k1)
    weight = jnp.where((rows_k == 0) | (rows_k == blocks), 1.0, 2.0)
    weight = jnp.where(rows_k < k1_true, weight, 0.0) / length
    ci, si = trig(blocks, k1, 2 * blocks)
    wi = jnp.concatenate([ci * weight[None, :], -si * weight[None, :]], axis=1)

    fields = jnp.concatenate([m_pos, g_pos, h_pos], axis=1)
    a = mm("ks,scr->kcr", w1, fields)
    are, aim = a[:k1], a[k1:]
    turned = jnp.concatenate([are * tw_c + aim * tw_s, aim * tw_c - are * tw_s], axis=2)
    spec = mm("kcn,nm->kcm", turned, w_fwd)

    mre, mim = spec[:, :cc, :lane], spec[:, :cc, lane:]
    gre, gim = spec[:, cc : 2 * cc, :lane], spec[:, cc : 2 * cc, lane:]
    h = spec[:, 2 * cc :]
    h = jnp.broadcast_to(h[:, :, None, :], (k1, per_dev, chan_n, 2 * lane)).reshape(k1, cc, 2 * lane)
    hre, him = h[:, :, :lane], h[:, :, lane:]

    conv_s = jnp.concatenate([hre * mre - him * mim, hre * mim + him * mre], axis=2)
    corr_s = jnp.concatenate([gre * hre + gim * him, gim * hre - gre * him], axis=2)
    taps_s = jnp.concatenate([gre * mre + gim * mim, gim * mre - gre * mim], axis=2)
    taps_s = jnp.sum(taps_s.reshape(k1, per_dev, chan_n, 2 * lane), axis=2)

    prod = jnp.concatenate([conv_s, corr_s, taps_s], axis=1)
    z = mm("kcn,nm->kcm", prod, w_inv)
    zre, zim = z[:, :, :lane], z[:, :, lane:]
    ure = zre * tw_c - zim * tw_s
    uim = zre * tw_s + zim * tw_c
    y = mm("ik,kcr->icr", wi, jnp.concatenate([ure, uim], axis=0))

    def by_chunk(block, copies):
        block = block.reshape(seq_n, qn, per_dev, copies, lane).transpose(0, 3, 2, 1, 4)
        return block.reshape(seq_n, copies, span)

    conv_blk = by_chunk(y[:, :cc], chan_n)
    corr_blk = by_chunk(y[:, cc : 2 * cc], chan_n)
    taps_blk = jnp.broadcast_to(by_chunk(y[:, 2 * cc :], 1), (seq_n, chan_n, span))
    skip_blk = jnp.broadcast_to(
        jnp.pad(skip_mine, ((0, 0), (0, pad_w - per_dev)))[None], (seq_n, chan_n, pad_w)
    )
    out_send = jnp.concatenate([conv_blk, corr_blk, taps_blk, skip_blk], axis=2)
    back = lax.all_to_all(out_send.reshape(dev_n, -1), ("seq", "chan"), 0, 0, tiled=True)

    def tail_kernel(bk, gi, vi, og, ot, sg, o_gg, o_gog, o_gv, o_taps, o_skip):
        def field(first):
            parts = [bk[pl.ds(first + q, dev_n, stride=back_w), :] for q in range(rq)]
            return jnp.concatenate(parts, axis=1).T

        for f2 in range(per_dev):
            lanes = pl.ds(f2 * dev_n, dev_n)
            conv = field(f2 * rq)
            corr = field((per_dev + f2) * rq)
            o_taps[:, lanes] = field((2 * per_dev + f2) * rq)
            gate = gi[:, lanes].astype(F32)
            val = vi[:, lanes].astype(F32)
            outg = og[:, lanes].astype(F32)
            m = (gate * val).astype(jnp.bfloat16).astype(F32)
            g = (outg * ot[:, lanes].astype(F32)).astype(jnp.bfloat16).astype(F32)
            s = sg[:, lanes]
            o_gog[:, lanes] = (outg * (conv + s * m)).astype(jnp.bfloat16)
            mix = corr + s * g
            o_gg[:, lanes] = (mix * val).astype(jnp.bfloat16)
            o_gv[:, lanes] = (mix * gate).astype(jnp.bfloat16)
        o_skip[...] = bk[pl.ds(3 * per_dev * rq, dev_n, stride=back_w), :].T[:per_dev, :]

    grad_shape = jax.ShapeDtypeStruct((rows, local_ch), jnp.bfloat16)
    grad_gate, grad_out_gate, grad_value, taps_grad, skip_two = pl.pallas_call(
        tail_kernel,
        out_shape=(
            grad_shape,
            grad_shape,
            grad_shape,
            jax.ShapeDtypeStruct((rows, filters), F32),
            jax.ShapeDtypeStruct((per_dev, dev_n), F32),
        ),
        cost_estimate=pl.CostEstimate(flops=12 * rows * local_ch, transcendentals=0, bytes_accessed=4 * 4 * rows * local_ch * 2),
    )(back.reshape(dev_n * back_w, lane), gate_in, value_in, out_grad, out_gate, skip_gain.reshape(1, local_ch))
    skip_grad = skip_two.reshape(local_ch)
    return (grad_gate, grad_out_gate, grad_value, skip_grad, taps_grad)


def solution(mesh):
    placed = (
        P("seq", "chan"),
        P("seq", "chan"),
        P("seq", "chan"),
        P("seq", "chan"),
        P("chan"),
        P("seq", None),
    )
    return jax.shard_map(
        body,
        mesh=mesh,
        in_specs=placed,
        out_specs=(P("seq", "chan"), P("seq", "chan"), P("seq", "chan"), P("chan"), P("seq", None)),
        check_vma=False,
    )
```
